256 devices in a mesh: wide: 32 (over y, x, core), narrow: 8 (over z).
Axes of the slice: x: 4, y: 4, z: 8, core: 2. Of those that a mesh axis runs over, the one named last changes fastest.
Arguments:
- up_grads: float32 [32, 192, 11008], P('wide', 'narrow'), may hold values from -6 to 6, as said below
- down_grads: float32 [32, 512, 4096], P('wide', 'narrow'), may hold values from -6 to 6, as said below
- gain_grads: float32 [32, 4096], P('wide', 'narrow'), may hold values from -6 to 6
- up_master: float32 [192, 11008], P('narrow', 'wide'), may hold values from -60 to 60, as said below
- down_master: float32 [512, 4096], P('narrow', 'wide'), may hold values from -60 to 60, as said below
- gain_master: float32 [4096], P(('narrow', 'wide')), may hold values from 0.5 to 1.5
- up_first: float32 [192, 11008], P('narrow', 'wide'), may hold values from -1.8 to 1.8, as said below
- down_first: float32 [512, 4096], P('narrow', 'wide'), may hold values from -1.8 to 1.8, as said below
- gain_first: float32 [4096], P(('narrow', 'wide')), may hold values from -4 to 4
- up_second: float32 [192, 11008], P('narrow', 'wide'), may hold values from 0.01 to 1
- down_second: float32 [512, 4096], P('narrow', 'wide'), may hold values from 0.01 to 1
- gain_second: float32 [4096], P(('narrow', 'wide')), may hold values from 0.01 to 1
Outputs:
- up_first_new: float32 [192, 11008], P('narrow', 'wide')
- up_second_new: float32 [192, 11008], P('narrow', 'wide')
- up_master_new: float32 [192, 11008], P('narrow', 'wide')
- up_weights: bfloat16 [192, 11008], replicated
- down_first_new: float32 [512, 4096], P('narrow', 'wide')
- down_second_new: float32 [512, 4096], P('narrow', 'wide')
- down_master_new: float32 [512, 4096], P('narrow', 'wide')
- down_weights: bfloat16 [512, 4096], replicated
- gain_first_new: float32 [4096], P(('narrow', 'wide'))
- gain_second_new: float32 [4096], P(('narrow', 'wide'))
- gain_master_new: float32 [4096], P(('narrow', 'wide'))
- gain_weights: bfloat16 [4096], replicated
The draws below stay inside these ranges and needn't reach their ends.
Inputs may be any that keep to these rules, and one draw needn't show every extreme that they name: `up_master`: finite real entries. `down_master`: finite real entries. `up_grads`: finite real entries. `down_grads`: finite real entries. `up_first`: finite real entries. `down_first`: finite real entries.
All inputs are finite; a program needn't handle non-finite values.
Results may differ from the reference program's by a relative error of at most 0.001.
Values may be sent and summed in bfloat16 or wider, within the bound.
No kernel may reach another device: no remote copies, remote signals or barrier semaphores. Data moves between devices by JAX's collectives and lax.ppermute only.
A program may use at most 64 MiB of HBM per device.

```python
import math
import jax
import jax.numpy as jnp
from jax import lax

D = 4096
FF = 11008
UP_ROWS = 192
DOWN_ROWS = 512
N_WIDE = 32
N_NARROW = 8


def scaled_matrix(key, rows, cols):
    keys = jax.random.split(key, 5)
    row_scale = jnp.exp(jax.random.uniform(keys[0], (rows, 1), jnp.float32, math.log(0.3), math.log(3.0)))
    col_scale = jnp.exp(jax.random.uniform(keys[1], (1, cols), jnp.float32, math.log(0.4), math.log(2.0)))
    row_place = jnp.arange(rows, dtype=jnp.float32).reshape(rows, 1) / rows - 0.5
    col_place = jnp.arange(cols, dtype=jnp.float32).reshape(1, cols) / cols - 0.5
    base = jnp.clip(jax.random.normal(keys[4], (rows, cols), jnp.float32), -6.0, 6.0)
    ramp = jnp.exp(math.log(2.0) * row_place) * jnp.exp(math.log(3.0) * col_place)
    return jnp.clip(base * row_scale * col_scale * ramp, -60.0, 60.0)


def block_spread(key, rows, cols, low, high):
    loud = jnp.exp(jax.random.uniform(key, (N_NARROW, N_WIDE), jnp.float32, math.log(low), math.log(high)))
    return jnp.repeat(jnp.repeat(loud, rows // N_NARROW, axis=0), cols // N_WIDE, axis=1)


def loud_grads(key, rows, cols):
    keys = jax.random.split(key, 4)
    spread = block_spread(keys[0], rows, cols, 0.02, 5.0)
    base = jnp.clip(jax.random.normal(keys[1], (N_WIDE, rows, cols), jnp.float32), -6.0, 6.0)
    order = jax.random.permutation(keys[3], N_WIDE)
    paired = (jnp.arange(N_WIDE)[None, :] == order[:, None]).astype(jnp.float32)
    spike = jnp.repeat(1.0 + 4.0 * paired, cols // N_WIDE, axis=1)
    return jnp.clip(0.2 * base * spread[None, :, :] * spike[:, None, :], -6.0, 6.0)


def loud_first(key, rows, cols):
    keys = jax.random.split(key, 3)
    column_loud = jnp.exp(jax.random.uniform(keys[0], (1, N_WIDE), jnp.float32, math.log(0.1), math.log(1.0)))
    column_loud = jnp.repeat(column_loud, cols // N_WIDE, axis=1)
    base = jnp.clip(jax.random.normal(keys[2], (rows, cols), jnp.float32), -6.0, 6.0)
    return jnp.clip(0.3 * base * column_loud, -1.8, 1.8)


def draw_up_master(key, part):
    return scaled_matrix(jax.random.fold_in(key, 11), UP_ROWS, FF)


def draw_down_master(key, part):
    return scaled_matrix(jax.random.fold_in(key, 23), DOWN_ROWS, D)


def draw_up_grads(key, part):
    return loud_grads(jax.random.fold_in(key, 37), UP_ROWS, FF)


def draw_down_grads(key, part):
    return loud_grads(jax.random.fold_in(key, 41), DOWN_ROWS, D)


def draw_up_first(key, part):
    return loud_first(jax.random.fold_in(key, 53), UP_ROWS, FF)


def draw_down_first(key, part):
    return loud_first(jax.random.fold_in(key, 67), DOWN_ROWS, D)


def spiked(array, rng, source, target, shards_of, factor):
    owner, partner = [(jnp.arange(array.shape[dim]) // (array.shape[dim] // shards_of)).reshape([-1 if axis == dim else 1 for axis in range(array.ndim)]) for dim in (source, target)]
    chosen = jax.random.permutation(rng, shards_of)[partner]
    strong = (owner == chosen) | (owner == (partner + shards_of // 2) % shards_of)
    return jnp.where(strong, factor * array, array)


def shard_levels(key, extent, pieces, low, largest):
    def one(axis_at, blocks):
        draws = jax.random.uniform(jax.random.fold_in(jax.random.fold_in(key, 6), axis_at), (blocks,), jnp.float32, low / len(pieces), largest / len(pieces))
        return jnp.repeat(jnp.exp(draws), extent[axis_at] // blocks).reshape((-1,) + (1,) * (len(extent) - axis_at - 1))

    factor_of = one(*pieces[0])
    for cut in pieces[1:]:
        factor_of = factor_of * one(*cut)
    return factor_of


def normal_values(stream_key, shape, scale, most, cuts=(), held_as=jnp.bfloat16):
    values = jax.random.normal(stream_key, shape, jnp.float32) * scale
    if len(cuts) > 0:
        values = shard_levels(stream_key, shape, cuts, -0.22, 0.18) * values
    return jnp.clip(values, min=-most, max=most).astype(held_as)


def bell_draw_with(rng, shape, scale, limit, pieces, heavy, held_as=jnp.bfloat16):
    result = scale * jax.random.normal(rng, shape, jnp.float32)
    if pieces:
        result = result * shard_levels(rng, shape, pieces, -0.22, 0.18)
    return jnp.clip(spiked(result, jax.random.fold_in(rng, 3), *heavy), -limit, limit).astype(held_as)


def setup_inputs(seed: int = 0) -> dict:
    splits = jax.random.split(jax.random.key(seed), 13)
    return {
        "up_grads": draw_up_grads(jax.random.fold_in(splits[12], 71), 0),
        "down_grads": draw_down_grads(jax.random.fold_in(splits[12], 71), 0),
        "gain_grads": bell_draw_with(splits[2], (N_WIDE, D), 0.2, 6.0, ((0, 32), (1, 8)), (0, 1, 32, 2.75), jnp.float32),
        "up_master": draw_up_master(jax.random.fold_in(splits[12], 71), 0),
        "down_master": draw_down_master(jax.random.fold_in(splits[12], 71), 0),
        "gain_master": jnp.clip(1.0 + 0.1 * jax.random.normal(splits[5], (D,), jnp.float32), 0.5, 1.5),
        "up_first": draw_up_first(jax.random.fold_in(splits[12], 71), 0),
        "down_first": draw_down_first(jax.random.fold_in(splits[12], 71), 0),
        "gain_first": normal_values(splits[8], (D,), 0.3, 4.0, ((0, 256),), jnp.float32),
        "up_second": jnp.clip(jnp.exp(math.log(1.0) - 4.6051702 * jax.random.uniform(splits[9], (UP_ROWS, FF), jnp.float32) ** shard_levels(splits[9], (UP_ROWS, FF), ((0, 8), (1, 32)), -0.2, 0.2)), 0.01, 1.0),
        "down_second": jnp.clip(jnp.exp(math.log(1.0) - 4.6051702 * jax.random.uniform(splits[10], (DOWN_ROWS, D), jnp.float32) ** shard_levels(splits[10], (DOWN_ROWS, D), ((0, 8), (1, 32)), -0.2, 0.2)), 0.01, 1.0),
        "gain_second": jnp.clip(jnp.exp(math.log(1.0) - 4.6051702 * jax.random.uniform(splits[11], (D,), jnp.float32) ** shard_levels(splits[11], (D,), ((0, 256),), -0.2, 0.2)), 0.01, 1.0),
    }


BETA_ONE = 0.9
BETA_TWO = 0.999
EPSILON = 1e-06
LEARN_RATE = 0.05
DECAY_RATE = 0.01
CORRECT_FIRST = 1.0 - 0.9 ** 10
CORRECT_SECOND = 1.0 - 0.999 ** 10

def adapt(grads, master, first, second, decay):
    grad_sum = lax.optimization_barrier(jnp.sum(grads, axis=0))
    first_new = BETA_ONE * first + (1.0 - BETA_ONE) * grad_sum
    second_new = BETA_TWO * second + (1.0 - BETA_TWO) * grad_sum * grad_sum
    update = first_new / CORRECT_FIRST / (jnp.sqrt(second_new / CORRECT_SECOND) + EPSILON) + decay * master
    weight_norm = jnp.sqrt(jnp.sum(master * master))
    update_norm = jnp.sqrt(jnp.sum(update * update))
    trust = weight_norm / (update_norm + EPSILON)
    master_new = master - LEARN_RATE * trust * update
    return (first_new, second_new, master_new, master_new.astype(jnp.bfloat16))

def reference(up_grads, down_grads, gain_grads, up_master, down_master, gain_master, up_first, down_first, gain_first, up_second, down_second, gain_second):
    up_out = adapt(up_grads, up_master, up_first, up_second, DECAY_RATE)
    down_out = adapt(down_grads, down_master, down_first, down_second, DECAY_RATE)
    gain_out = adapt(gain_grads, gain_master, gain_first, gain_second, 0.0)
    return (up_out[0], up_out[1], up_out[2], up_out[3], down_out[0], down_out[1], down_out[2], down_out[3], gain_out[0], gain_out[1], gain_out[2], gain_out[3])
```

```python
import jax
import jax.numpy as jnp
from jax import lax
from jax.sharding import PartitionSpec as P

BETA_ONE = 0.9
BETA_TWO = 0.999
EPSILON = 1e-06
LEARN_RATE = 0.05
DECAY_RATE = 0.01
CORRECT_FIRST = 1.0 - 0.9**10
CORRECT_SECOND = 1.0 - 0.999**10
LANES = 128


def moments(grad_sum, master, first, second, decay):
    first_new = BETA_ONE * first + (1.0 - BETA_ONE) * grad_sum
    second_new = BETA_TWO * second + (1.0 - BETA_TWO) * grad_sum * grad_sum
    update = (
        first_new / CORRECT_FIRST / (jnp.sqrt(second_new / CORRECT_SECOND) + EPSILON)
        + decay * master
    )
    return (first_new, second_new, update)


def finish(master, update, weight_sq, update_sq):
    trust = jnp.sqrt(weight_sq) / (jnp.sqrt(update_sq) + EPSILON)
    return master - LEARN_RATE * trust * update


def padded(total):
    return -(-total // LANES) * LANES


def body(
    up_grads,
    down_grads,
    gain_grads,
    up_master,
    down_master,
    gain_master,
    up_first,
    down_first,
    gain_first,
    up_second,
    down_second,
    gain_second,
):
    n_wide = lax.axis_size("wide")
    n_narrow = lax.axis_size("narrow")
    up_rows, up_cols = up_master.shape
    down_rows, down_cols = down_master.shape
    gain_cols = gain_master.shape[0]
    up_size = up_rows * up_cols
    down_size = down_rows * down_cols
    total = up_size + down_size + gain_cols
    width = padded(total)

    weight_sums = (
        jnp.sum(up_master * up_master),
        jnp.sum(down_master * down_master),
        jnp.sum(gain_master * gain_master),
    )

    up_part = up_grads[0].reshape(up_rows, n_wide, up_cols).transpose(1, 0, 2)
    down_part = down_grads[0].reshape(down_rows, n_wide, down_cols).transpose(1, 0, 2)
    gain_part = gain_grads.reshape(n_wide, gain_cols)
    packed = jnp.concatenate(
        [
            up_part.reshape(n_wide, up_size),
            down_part.reshape(n_wide, down_size),
            gain_part,
            jnp.zeros((n_wide, width - total), jnp.float32),
        ],
        axis=1,
    ).reshape(n_wide, width // LANES, LANES)
    summed = lax.psum_scatter(packed, "wide", scatter_dimension=0, tiled=True)
    summed = summed.reshape(width)
    up_sum = summed[:up_size].reshape(up_rows, up_cols)
    down_sum = summed[up_size : up_size + down_size].reshape(down_rows, down_cols)
    gain_sum = summed[up_size + down_size : total]

    up_first_new, up_second_new, up_update = moments(
        up_sum, up_master, up_first, up_second, DECAY_RATE
    )
    down_first_new, down_second_new, down_update = moments(
        down_sum, down_master, down_first, down_second, DECAY_RATE
    )
    gain_first_new, gain_second_new, gain_update = moments(
        gain_sum, gain_master, gain_first, gain_second, 0.0
    )
    weight_sums, update_sums = lax.psum(
        (
            weight_sums,
            (
                jnp.sum(up_update * up_update),
                jnp.sum(down_update * down_update),
                jnp.sum(gain_update * gain_update),
            ),
        ),
        ("wide", "narrow"),
    )
    up_master_new = finish(up_master, up_update, weight_sums[0], update_sums[0])
    down_master_new = finish(down_master, down_update, weight_sums[1], update_sums[1])
    gain_master_new = finish(gain_master, gain_update, weight_sums[2], update_sums[2])

    low = jnp.concatenate(
        [
            up_master_new.astype(jnp.bfloat16).reshape(up_size),
            down_master_new.astype(jnp.bfloat16).reshape(down_size),
            gain_master_new.astype(jnp.bfloat16),
            jnp.zeros((width - total,), jnp.bfloat16),
        ]
    ).reshape(1, width // LANES, LANES)
    whole = lax.all_gather(low, ("narrow", "wide"), axis=0, tiled=True)
    whole = whole.reshape(n_narrow, n_wide, width)
    up_weights = (
        whole[:, :, :up_size]
        .reshape(n_narrow, n_wide, up_rows, up_cols)
        .transpose(0, 2, 1, 3)
        .reshape(n_narrow * up_rows, n_wide * up_cols)
    )
    down_weights = (
        whole[:, :, up_size : up_size + down_size]
        .reshape(n_narrow, n_wide, down_rows, down_cols)
        .transpose(0, 2, 1, 3)
        .reshape(n_narrow * down_rows, n_wide * down_cols)
    )
    gain_weights = whole[:, :, up_size + down_size : total].reshape(-1)
    return (
        up_first_new,
        up_second_new,
        up_master_new,
        up_weights,
        down_first_new,
        down_second_new,
        down_master_new,
        down_weights,
        gain_first_new,
        gain_second_new,
        gain_master_new,
        gain_weights,
    )


def solution(mesh):
    return jax.shard_map(
        body,
        mesh=mesh,
        in_specs=(
            P("wide", "narrow", None),
            P("wide", "narrow", None),
            P("wide", "narrow"),
            P("narrow", "wide"),
            P("narrow", "wide"),
            P(("narrow", "wide")),
            P("narrow", "wide"),
            P("narrow", "wide"),
            P(("narrow", "wide")),
            P("narrow", "wide"),
            P("narrow", "wide"),
            P(("narrow", "wide")),
        ),
        out_specs=(
            P("narrow", "wide"),
            P("narrow", "wide"),
            P("narrow", "wide"),
            P(),
            P("narrow", "wide"),
            P("narrow", "wide"),
            P("narrow", "wide"),
            P(),
            P(("narrow", "wide")),
            P(("narrow", "wide")),
            P(("narrow", "wide")),
            P(),
        ),
        check_vma=False,
    )
```

```python
import jax
import jax.numpy as jnp
from jax import lax
from jax.sharding import PartitionSpec as P

BETA_ONE = 0.9
BETA_TWO = 0.999
EPSILON = 1e-06
LEARN_RATE = 0.05
DECAY_RATE = 0.01
CORRECT_FIRST = 1.0 - 0.9**10
CORRECT_SECOND = 1.0 - 0.999**10
LANES = 128


def moments(grad_sum, master, first, second, decay):
    first_new = BETA_ONE * first + (1.0 - BETA_ONE) * grad_sum
    second_new = BETA_TWO * second + (1.0 - BETA_TWO) * grad_sum * grad_sum
    update = (
        first_new / CORRECT_FIRST / (jnp.sqrt(second_new / CORRECT_SECOND) + EPSILON)
        + decay * master
    )
    return (first_new, second_new, update)


def finish(master, update, weight_sq, update_sq):
    trust = jnp.sqrt(weight_sq) / (jnp.sqrt(update_sq) + EPSILON)
    return master - LEARN_RATE * trust * update


def butterfly_sum(x, n_wide, n_narrow):
    for axis, size in (("wide", n_wide), ("narrow", n_narrow)):
        step = 1
        while step < size:
            pairs = [(i, i ^ step) for i in range(size)]
            x = x + lax.ppermute(x, axis, pairs)
            step *= 2
    return x


def body(
    up_grads,
    down_grads,
    gain_grads,
    up_master,
    down_master,
    gain_master,
    up_first,
    down_first,
    gain_first,
    up_second,
    down_second,
    gain_second,
):
    n_wide = lax.axis_size("wide")
    n_narrow = lax.axis_size("narrow")
    up_rows, up_cols = up_master.shape
    down_rows, down_cols = down_master.shape
    gain_cols = gain_master.shape[0]
    up_tiles = -(-up_cols // LANES)
    up_pad = up_tiles * LANES
    up_at = down_rows
    gain_at = up_at + up_rows * up_tiles
    height = -(-(gain_at + 1) // 16) * 16

    down_part = down_grads[0].reshape(down_rows, n_wide, down_cols).transpose(1, 0, 2)
    up_part = up_grads[0].reshape(up_rows, n_wide, up_cols)
    up_part = jnp.pad(up_part, ((0, 0), (0, 0), (0, up_pad - up_cols)))
    up_part = up_part.reshape(up_rows, n_wide, up_tiles, LANES).transpose(1, 0, 2, 3)
    up_part = up_part.reshape(n_wide, up_rows * up_tiles, LANES)
    gain_part = jnp.pad(gain_grads.reshape(n_wide, 1, gain_cols), ((0, 0), (0, 0), (0, LANES - gain_cols)))
    packed = jnp.concatenate(
        [
            down_part,
            up_part,
            gain_part,
            jnp.zeros((n_wide, height - gain_at - 1, LANES), jnp.float32),
        ],
        axis=1,
    )
    received = lax.all_to_all(packed, "wide", 0, 0, tiled=True)
    summed = jnp.sum(received, axis=0)
    down_sum = summed[:down_rows]
    up_sum = summed[up_at:gain_at].reshape(up_rows, up_pad)[:, :up_cols]
    gain_sum = summed[gain_at, :gain_cols]

    up_first_new, up_second_new, up_update = moments(
        up_sum, up_master, up_first, up_second, DECAY_RATE
    )
    down_first_new, down_second_new, down_update = moments(
        down_sum, down_master, down_first, down_second, DECAY_RATE
    )
    gain_first_new, gain_second_new, gain_update = moments(
        gain_sum, gain_master, gain_first, gain_second, 0.0
    )
    partial = jnp.stack(
        [
            jnp.sum(up_master * up_master),
            jnp.sum(down_master * down_master),
            jnp.sum(gain_master * gain_master),
            jnp.sum(up_update * up_update),
            jnp.sum(down_update * down_update),
            jnp.sum(gain_update * gain_update),
            jnp.float32(0.0),
            jnp.float32(0.0),
        ]
    )
    sums = butterfly_sum(partial, n_wide, n_narrow)
    up_master_new = finish(up_master, up_update, sums[0], sums[3])
    down_master_new = finish(down_master, down_update, sums[1], sums[4])
    gain_master_new = finish(gain_master, gain_update, sums[2], sums[5])

    up_low = jnp.pad(up_master_new.astype(jnp.bfloat16), ((0, 0), (0, up_pad - up_cols)))
    low = jnp.concatenate(
        [
            down_master_new.astype(jnp.bfloat16),
            up_low.reshape(up_rows * up_tiles, LANES),
            jnp.pad(gain_master_new.astype(jnp.bfloat16), (0, LANES - gain_cols)).reshape(1, LANES),
            jnp.zeros((height - gain_at - 1, LANES), jnp.bfloat16),
        ]
    )
    rows = lax.all_to_all(
        jnp.broadcast_to(low[None], (n_narrow, height, LANES)), "narrow", 0, 0, tiled=True
    )
    whole = lax.all_gather(rows[None], "wide", axis=0, tiled=True)
    down_weights = (
        whole[:, :, :down_rows]
        .transpose(1, 2, 0, 3)
        .reshape(n_narrow * down_rows, n_wide * down_cols)
    )
    up_weights = (
        whole[:, :, up_at:gain_at]
        .reshape(n_wide, n_narrow, up_rows, up_tiles, LANES)
        .transpose(1, 2, 0, 3, 4)
        .reshape(n_narrow, up_rows, n_wide, up_pad)[:, :, :, :up_cols]
        .reshape(n_narrow * up_rows, n_wide * up_cols)
    )
    gain_weights = whole[:, :, gain_at, :gain_cols].transpose(1, 0, 2).reshape(-1)
    return (
        up_first_new,
        up_second_new,
        up_master_new,
        up_weights,
        down_first_new,
        down_second_new,
        down_master_new,
        down_weights,
        gain_first_new,
        gain_second_new,
        gain_master_new,
        gain_weights,
    )


def solution(mesh):
    return jax.shard_map(
        body,
        mesh=mesh,
        in_specs=(
            P("wide", "narrow", None),
            P("wide", "narrow", None),
            P("wide", "narrow"),
            P("narrow", "wide"),
            P("narrow", "wide"),
            P(("narrow", "wide")),
            P("narrow", "wide"),
            P("narrow", "wide"),
            P(("narrow", "wide")),
            P("narrow", "wide"),
            P("narrow", "wide"),
            P(("narrow", "wide")),
        ),
        out_specs=(
            P("narrow", "wide"),
            P("narrow", "wide"),
            P("narrow", "wide"),
            P(),
            P("narrow", "wide"),
            P("narrow", "wide"),
            P("narrow", "wide"),
            P(),
            P(("narrow", "wide")),
            P(("narrow", "wide")),
            P(("narrow", "wide")),
            P(),
        ),
        check_vma=False,
    )
```

```python
import jax
import jax.numpy as jnp
from jax import lax
from jax.sharding import PartitionSpec as P

BETA_ONE = 0.9
BETA_TWO = 0.999
EPSILON = 1e-06
LEARN_RATE = 0.05
DECAY_RATE = 0.01
CORRECT_FIRST = 1.0 - 0.9**10
CORRECT_SECOND = 1.0 - 0.999**10
LANES = 128


def moments(grad_sum, master, first, second, decay):
    first_new = BETA_ONE * first + (1.0 - BETA_ONE) * grad_sum
    second_new = BETA_TWO * second + (1.0 - BETA_TWO) * grad_sum * grad_sum
    update = (
        first_new / CORRECT_FIRST / (jnp.sqrt(second_new / CORRECT_SECOND) + EPSILON)
        + decay * master
    )
    return (first_new, second_new, update)


def finish(master, update, weight_sq, update_sq):
    trust = jnp.sqrt(weight_sq) / (jnp.sqrt(update_sq) + EPSILON)
    return master - LEARN_RATE * trust * update


def butterfly_sum(x, n_wide, n_narrow):
    for axis, size in (("wide", n_wide), ("narrow", n_narrow)):
        step = 1
        while step < size:
            pairs = [(i, i ^ step) for i in range(size)]
            x = x + lax.ppermute(x, axis, pairs)
            step *= 2
    return x


def body(
    up_grads,
    down_grads,
    gain_grads,
    up_master,
    down_master,
    gain_master,
    up_first,
    down_first,
    gain_first,
    up_second,
    down_second,
    gain_second,
):
    n_wide = lax.axis_size("wide")
    n_narrow = lax.axis_size("narrow")
    up_rows, up_cols = up_master.shape
    down_rows, down_cols = down_master.shape
    gain_cols = gain_master.shape[0]
    up_tiles = -(-up_cols // LANES)
    up_pad = up_tiles * LANES
    up_at = down_rows
    gain_at = up_at + up_rows * up_tiles
    height = -(-(gain_at + 1) // 16) * 16

    down_part = down_grads[0].reshape(down_rows, n_wide, down_cols).transpose(1, 0, 2)
    up_part = up_grads[0].reshape(up_rows, n_wide, up_cols)
    up_part = jnp.pad(up_part, ((0, 0), (0, 0), (0, up_pad - up_cols)))
    up_part = up_part.reshape(up_rows, n_wide, up_tiles, LANES).transpose(1, 0, 2, 3)
    up_part = up_part.reshape(n_wide, up_rows * up_tiles, LANES)
    gain_part = jnp.pad(gain_grads.reshape(n_wide, 1, gain_cols), ((0, 0), (0, 0), (0, LANES - gain_cols)))
    packed = jnp.concatenate(
        [
            down_part,
            up_part,
            gain_part,
            jnp.zeros((n_wide, height - gain_at - 1, LANES), jnp.float32),
        ],
        axis=1,
    )
    received = lax.all_to_all(packed, "wide", 0, 0, tiled=True)
    summed = jnp.sum(received, axis=0)
    down_sum = summed[:down_rows]
    up_sum = summed[up_at:gain_at].reshape(up_rows, up_pad)[:, :up_cols]
    gain_sum = summed[gain_at, :gain_cols]

    up_first_new, up_second_new, up_update = moments(
        up_sum, up_master, up_first, up_second, DECAY_RATE
    )
    down_first_new, down_second_new, down_update = moments(
        down_sum, down_master, down_first, down_second, DECAY_RATE
    )
    gain_first_new, gain_second_new, gain_update = moments(
        gain_sum, gain_master, gain_first, gain_second, 0.0
    )
    partial = jnp.stack(
        [
            jnp.sum(up_master * up_master),
            jnp.sum(down_master * down_master),
            jnp.sum(gain_master * gain_master),
            jnp.sum(up_update * up_update),
            jnp.sum(down_update * down_update),
            jnp.sum(gain_update * gain_update),
            jnp.float32(0.0),
            jnp.float32(0.0),
        ]
    )
    sums = butterfly_sum(partial, n_wide, n_narrow)
    up_master_new = finish(up_master, up_update, sums[0], sums[3])
    down_master_new = finish(down_master, down_update, sums[1], sums[4])
    gain_master_new = finish(gain_master, gain_update, sums[2], sums[5])

    up_low = jnp.pad(up_master_new.astype(jnp.bfloat16), ((0, 0), (0, up_pad - up_cols)))
    down_low = down_master_new.astype(jnp.bfloat16).reshape(4, 16, LANES)
    gain_low = jnp.pad(gain_master_new.astype(jnp.bfloat16), (0, LANES - gain_cols))
    gain_low = jnp.pad(gain_low.reshape(1, LANES), ((0, 15), (0, 0)))
    down_area = jnp.concatenate(
        [
            jnp.concatenate([down_low[0], down_low[1], down_low[2]], axis=1),
            jnp.concatenate([down_low[3], gain_low, jnp.zeros((16, LANES), jnp.bfloat16)], axis=1),
        ]
    )
    low = jnp.concatenate(
        [up_low, jnp.zeros((32 - up_rows, up_pad), jnp.bfloat16), down_area]
    )
    rows = lax.all_to_all(
        jnp.broadcast_to(low[None], (n_narrow,) + low.shape), "narrow", 0, 0, tiled=True
    )
    whole = lax.all_gather(rows[None], "wide", axis=0, tiled=True)
    up_weights = (
        whole[:, :, :up_rows, :up_cols]
        .transpose(1, 2, 0, 3)
        .reshape(n_narrow * up_rows, n_wide * up_cols)
    )
    down_tiles = jnp.concatenate(
        [
            whole[:, :, 32:48, 0:128],
            whole[:, :, 32:48, 128:256],
            whole[:, :, 32:48, 256:384],
            whole[:, :, 48:64, 0:128],
        ],
        axis=2,
    )
    down_weights = down_tiles.transpose(1, 2, 0, 3).reshape(n_narrow * down_rows, n_wide * down_cols)
    gain_weights = whole[:, :, 48, 128 : 128 + gain_cols].transpose(1, 0, 2).reshape(-1)
    return (
        up_first_new,
        up_second_new,
        up_master_new,
        up_weights,
        down_first_new,
        down_second_new,
        down_master_new,
        down_weights,
        gain_first_new,
        gain_second_new,
        gain_master_new,
        gain_weights,
    )


def solution(mesh):
    return jax.shard_map(
        body,
        mesh=mesh,
        in_specs=(
            P("wide", "narrow", None),
            P("wide", "narrow", None),
            P("wide", "narrow"),
            P("narrow", "wide"),
            P("narrow", "wide"),
            P(("narrow", "wide")),
            P("narrow", "wide"),
            P("narrow", "wide"),
            P(("narrow", "wide")),
            P("narrow", "wide"),
            P("narrow", "wide"),
            P(("narrow", "wide")),
        ),
        out_specs=(
            P("narrow", "wide"),
            P("narrow", "wide"),
            P("narrow", "wide"),
            P(),
            P("narrow", "wide"),
            P("narrow", "wide"),
            P("narrow", "wide"),
            P(),
            P(("narrow", "wide")),
            P(("narrow", "wide")),
            P(("narrow", "wide")),
            P(),
        ),
        check_vma=False,
    )
```

```python
import jax
import jax.numpy as jnp
from jax import lax
from jax.sharding import PartitionSpec as P

BETA_ONE = 0.9
BETA_TWO = 0.999
EPSILON = 1e-06
LEARN_RATE = 0.05
DECAY_RATE = 0.01
CORRECT_FIRST = 1.0 - 0.9**10
CORRECT_SECOND = 1.0 - 0.999**10
LANES = 128


def moments(grad_sum, master, first, second, decay):
    first_new = BETA_ONE * first + (1.0 - BETA_ONE) * grad_sum
    second_new = BETA_TWO * second + (1.0 - BETA_TWO) * grad_sum * grad_sum
    update = (
        first_new / CORRECT_FIRST / (jnp.sqrt(second_new / CORRECT_SECOND) + EPSILON)
        + decay * master
    )
    return (first_new, second_new, update)


def finish(master, update, weight_sq, update_sq):
    trust = jnp.sqrt(weight_sq) / (jnp.sqrt(update_sq) + EPSILON)
    return master - LEARN_RATE * trust * update


def group_sum(x, axis, masks):
    size = lax.axis_size(axis)
    got = [lax.ppermute(x, axis, [(i, i ^ m) for i in range(size)]) for m in masks]
    while len(got) > 1:
        got = [got[i] + got[i + 1] if i + 1 < len(got) else got[i] for i in range(0, len(got), 2)]
    return x + got[0]


def mesh_sum(x):
    x = group_sum(x, "wide", (1,))
    x = group_sum(x, "wide", (2, 4, 6))
    x = group_sum(x, "wide", (8, 16, 24))
    return group_sum(x, "narrow", tuple(range(1, lax.axis_size("narrow"))))


def body(
    up_grads,
    down_grads,
    gain_grads,
    up_master,
    down_master,
    gain_master,
    up_first,
    down_first,
    gain_first,
    up_second,
    down_second,
    gain_second,
):
    n_wide = lax.axis_size("wide")
    n_narrow = lax.axis_size("narrow")
    up_rows, up_cols = up_master.shape
    down_rows, down_cols = down_master.shape
    gain_cols = gain_master.shape[0]
    up_tiles = -(-up_cols // LANES)
    up_pad = up_tiles * LANES
    up_at = down_rows
    gain_at = up_at + up_rows * up_tiles
    height = -(-(gain_at + 1) // 16) * 16

    down_part = down_grads[0].reshape(down_rows, n_wide, down_cols).transpose(1, 0, 2)
    up_part = up_grads[0].reshape(up_rows, n_wide, up_cols)
    up_part = jnp.pad(up_part, ((0, 0), (0, 0), (0, up_pad - up_cols)))
    up_part = up_part.reshape(up_rows, n_wide, up_tiles, LANES).transpose(1, 0, 2, 3)
    up_part = up_part.reshape(n_wide, up_rows * up_tiles, LANES)
    gain_part = jnp.pad(gain_grads.reshape(n_wide, 1, gain_cols), ((0, 0), (0, 0), (0, LANES - gain_cols)))
    packed = jnp.concatenate(
        [
            down_part,
            up_part,
            gain_part,
            jnp.zeros((n_wide, height - gain_at - 1, LANES), jnp.float32),
        ],
        axis=1,
    )
    received = lax.all_to_all(packed, "wide", 0, 0, tiled=True)
    summed = jnp.sum(received, axis=0)
    down_sum = summed[:down_rows]
    up_sum = summed[up_at:gain_at].reshape(up_rows, up_pad)[:, :up_cols]
    gain_sum = summed[gain_at, :gain_cols]

    up_first_new, up_second_new, up_update = moments(
        up_sum, up_master, up_first, up_second, DECAY_RATE
    )
    down_first_new, down_second_new, down_update = moments(
        down_sum, down_master, down_first, down_second, DECAY_RATE
    )
    gain_first_new, gain_second_new, gain_update = moments(
        gain_sum, gain_master, gain_first, gain_second, 0.0
    )
    partial = jnp.stack(
        [
            jnp.sum(up_master * up_master),
            jnp.sum(down_master * down_master),
            jnp.sum(gain_master * gain_master),
            jnp.sum(up_update * up_update),
            jnp.sum(down_update * down_update),
            jnp.sum(gain_update * gain_update),
            jnp.float32(0.0),
            jnp.float32(0.0),
        ]
    )
    sums = mesh_sum(partial)
    up_master_new = finish(up_master, up_update, sums[0], sums[3])
    down_master_new = finish(down_master, down_update, sums[1], sums[4])
    gain_master_new = finish(gain_master, gain_update, sums[2], sums[5])

    up_low = jnp.pad(up_master_new.astype(jnp.bfloat16), ((0, 0), (0, up_pad - up_cols)))
    down_low = down_master_new.astype(jnp.bfloat16).reshape(4, 16, LANES)
    gain_low = jnp.pad(gain_master_new.astype(jnp.bfloat16), (0, LANES - gain_cols))
    gain_low = jnp.pad(gain_low.reshape(1, LANES), ((0, 15), (0, 0)))
    down_area = jnp.concatenate(
        [
            jnp.concatenate([down_low[0], down_low[1], down_low[2]], axis=1),
            jnp.concatenate([down_low[3], gain_low, jnp.zeros((16, LANES), jnp.bfloat16)], axis=1),
        ]
    )
    low = jnp.concatenate(
        [up_low, jnp.zeros((32 - up_rows, up_pad), jnp.bfloat16), down_area]
    )
    rows = lax.all_to_all(
        jnp.broadcast_to(low[None], (n_narrow,) + low.shape), "narrow", 0, 0, tiled=True
    )
    whole = lax.all_gather(rows[None], "wide", axis=0, tiled=True)
    up_weights = (
        whole[:, :, :up_rows, :up_cols]
        .transpose(1, 2, 0, 3)
        .reshape(n_narrow * up_rows, n_wide * up_cols)
    )
    down_tiles = jnp.concatenate(
        [
            whole[:, :, 32:48, 0:128],
            whole[:, :, 32:48, 128:256],
            whole[:, :, 32:48, 256:384],
            whole[:, :, 48:64, 0:128],
        ],
        axis=2,
    )
    down_weights = down_tiles.transpose(1, 2, 0, 3).reshape(n_narrow * down_rows, n_wide * down_cols)
    gain_weights = whole[:, :, 48, 128 : 128 + gain_cols].transpose(1, 0, 2).reshape(-1)
    return (
        up_first_new,
        up_second_new,
        up_master_new,
        up_weights,
        down_first_new,
        down_second_new,
        down_master_new,
        down_weights,
        gain_first_new,
        gain_second_new,
        gain_master_new,
        gain_weights,
    )


def solution(mesh):
    return jax.shard_map(
        body,
        mesh=mesh,
        in_specs=(
            P("wide", "narrow", None),
            P("wide", "narrow", None),
            P("wide", "narrow"),
            P("narrow", "wide"),
            P("narrow", "wide"),
            P(("narrow", "wide")),
            P("narrow", "wide"),
            P("narrow", "wide"),
            P(("narrow", "wide")),
            P("narrow", "wide"),
            P("narrow", "wide"),
            P(("narrow", "wide")),
        ),
        out_specs=(
            P("narrow", "wide"),
            P("narrow", "wide"),
            P("narrow", "wide"),
            P(),
            P("narrow", "wide"),
            P("narrow", "wide"),
            P("narrow", "wide"),
            P(),
            P(("narrow", "wide")),
            P(("narrow", "wide")),
            P(("narrow", "wide")),
            P(),
        ),
        check_vma=False,
    )
```

```python
import jax
import jax.numpy as jnp
from jax import lax
from jax.sharding import PartitionSpec as P
from jax.experimental import pallas as pl
from jax.experimental.pallas import tpu as pltpu

BETA_ONE = 0.9
BETA_TWO = 0.999
EPSILON = 1e-06
LEARN_RATE = 0.05
DECAY_RATE = 0.01
CORRECT_FIRST = 1.0 - 0.9**10
CORRECT_SECOND = 1.0 - 0.999**10
LANES = 128


def moments(grad_sum, master, first, second, decay):
    first_new = BETA_ONE * first + (1.0 - BETA_ONE) * grad_sum
    second_new = BETA_TWO * second + (1.0 - BETA_TWO) * grad_sum * grad_sum
    update = (
        first_new / CORRECT_FIRST / (jnp.sqrt(second_new / CORRECT_SECOND) + EPSILON)
        + decay * master
    )
    return (first_new, second_new, update)


def finish(master, update, weight_sq, update_sq):
    trust = jnp.sqrt(weight_sq) / (jnp.sqrt(update_sq) + EPSILON)
    return master - LEARN_RATE * trust * update


def group_sum(x, axis, masks):
    size = lax.axis_size(axis)
    got = [lax.ppermute(x, axis, [(i, i ^ m) for i in range(size)]) for m in masks]
    while len(got) > 1:
        got = [got[i] + got[i + 1] if i + 1 < len(got) else got[i] for i in range(0, len(got), 2)]
    return x + got[0]


def mesh_sum(x):
    x = group_sum(x, "wide", (1,))
    x = group_sum(x, "wide", (2, 4, 6))
    x = group_sum(x, "wide", (8, 16, 24))
    step = 1
    while step < lax.axis_size("narrow"):
        x = group_sum(x, "narrow", (step,))
        step *= 2
    return x


def unpack(whole, up_shape, down_shape):
    n_wide, n_narrow, height, width = whole.shape
    up_rows, up_cols = up_shape
    down_rows, down_cols = down_shape
    per = 2

    def kernel(in_ref, up_ref, down_ref):
        for j in range(per):
            for w in range(n_wide):
                up_ref[up_rows * j : up_rows * (j + 1), up_cols * w : up_cols * (w + 1)] = in_ref[
                    w, j, :up_rows, :up_cols
                ]
                for t in range(down_rows // 16):
                    row = 32 + 16 * (t // 3)
                    lane = LANES * (t % 3)
                    down_ref[
                        down_rows * j + 16 * t : down_rows * j + 16 * (t + 1),
                        down_cols * w : down_cols * (w + 1),
                    ] = in_ref[w, j, row : row + 16, lane : lane + LANES]

    moved = whole.size * 2 + (up_rows * up_cols + down_rows * down_cols) * n_wide * n_narrow * 2
    return pl.pallas_call(
        kernel,
        grid=(n_narrow // per,),
        in_specs=[pl.BlockSpec((n_wide, per, height, width), lambda i: (0, i, 0, 0))],
        out_specs=[
            pl.BlockSpec((per * up_rows, n_wide * up_cols), lambda i: (i, 0)),
            pl.BlockSpec((per * down_rows, n_wide * down_cols), lambda i: (i, 0)),
        ],
        out_shape=[
            jax.ShapeDtypeStruct((n_narrow * up_rows, n_wide * up_cols), jnp.bfloat16),
            jax.ShapeDtypeStruct((n_narrow * down_rows, n_wide * down_cols), jnp.bfloat16),
        ],
        cost_estimate=pl.CostEstimate(flops=0, transcendentals=0, bytes_accessed=moved),
    )(whole)


def body(
    up_grads,
    down_grads,
    gain_grads,
    up_master,
    down_master,
    gain_master,
    up_first,
    down_first,
    gain_first,
    up_second,
    down_second,
    gain_second,
):
    n_wide = lax.axis_size("wide")
    n_narrow = lax.axis_size("narrow")
    up_rows, up_cols = up_master.shape
    down_rows, down_cols = down_master.shape
    gain_cols = gain_master.shape[0]
    up_tiles = -(-up_cols // LANES)
    up_pad = up_tiles * LANES
    up_at = down_rows
    gain_at = up_at + up_rows * up_tiles
    height = -(-(gain_at + 1) // 16) * 16

    down_part = down_grads[0].reshape(down_rows, n_wide, down_cols).transpose(1, 0, 2)
    up_part = up_grads[0].reshape(up_rows, n_wide, up_cols)
    up_part = jnp.pad(up_part, ((0, 0), (0, 0), (0, up_pad - up_cols)))
    up_part = up_part.reshape(up_rows, n_wide, up_tiles, LANES).transpose(1, 0, 2, 3)
    up_part = up_part.reshape(n_wide, up_rows * up_tiles, LANES)
    gain_part = jnp.pad(gain_grads.reshape(n_wide, 1, gain_cols), ((0, 0), (0, 0), (0, LANES - gain_cols)))
    packed = jnp.concatenate(
        [
            down_part,
            up_part,
            gain_part,
            jnp.zeros((n_wide, height - gain_at - 1, LANES), jnp.float32),
        ],
        axis=1,
    )
    received = lax.all_to_all(packed, "wide", 0, 0, tiled=True)
    summed = jnp.sum(received, axis=0)
    down_sum = summed[:down_rows]
    up_sum = summed[up_at:gain_at].reshape(up_rows, up_pad)[:, :up_cols]
    gain_sum = summed[gain_at, :gain_cols]

    up_first_new, up_second_new, up_update = moments(
        up_sum, up_master, up_first, up_second, DECAY_RATE
    )
    down_first_new, down_second_new, down_update = moments(
        down_sum, down_master, down_first, down_second, DECAY_RATE
    )
    gain_first_new, gain_second_new, gain_update = moments(
        gain_sum, gain_master, gain_first, gain_second, 0.0
    )
    partial = jnp.stack(
        [
            jnp.sum(up_master * up_master),
            jnp.sum(down_master * down_master),
            jnp.sum(gain_master * gain_master),
            jnp.sum(up_update * up_update),
            jnp.sum(down_update * down_update),
            jnp.sum(gain_update * gain_update),
            jnp.float32(0.0),
            jnp.float32(0.0),
        ]
    )
    sums = mesh_sum(partial)
    up_master_new = finish(up_master, up_update, sums[0], sums[3])
    down_master_new = finish(down_master, down_update, sums[1], sums[4])
    gain_master_new = finish(gain_master, gain_update, sums[2], sums[5])

    up_low = jnp.pad(up_master_new.astype(jnp.bfloat16), ((0, 0), (0, up_pad - up_cols)))
    down_low = down_master_new.astype(jnp.bfloat16).reshape(4, 16, LANES)
    gain_low = jnp.pad(gain_master_new.astype(jnp.bfloat16), (0, LANES - gain_cols))
    gain_low = jnp.pad(gain_low.reshape(1, LANES), ((0, 15), (0, 0)))
    down_area = jnp.concatenate(
        [
            jnp.concatenate([down_low[0], down_low[1], down_low[2]], axis=1),
            jnp.concatenate([down_low[3], gain_low, jnp.zeros((16, LANES), jnp.bfloat16)], axis=1),
        ]
    )
    low = jnp.concatenate(
        [up_low, jnp.zeros((32 - up_rows, up_pad), jnp.bfloat16), down_area]
    )
    rows = lax.all_to_all(
        jnp.broadcast_to(low[None], (n_narrow,) + low.shape), "narrow", 0, 0, tiled=True
    )
    whole = lax.all_gather(rows[None], "wide", axis=0, tiled=True)
    up_weights, down_weights = unpack(whole, up_master.shape, down_master.shape)
    gain_weights = whole[:, :, 48, 128 : 128 + gain_cols].transpose(1, 0, 2).reshape(-1)
    return (
        up_first_new,
        up_second_new,
        up_master_new,
        up_weights,
        down_first_new,
        down_second_new,
        down_master_new,
        down_weights,
        gain_first_new,
        gain_second_new,
        gain_master_new,
        gain_weights,
    )


def solution(mesh):
    return jax.shard_map(
        body,
        mesh=mesh,
        in_specs=(
            P("wide", "narrow", None),
            P("wide", "narrow", None),
            P("wide", "narrow"),
            P("narrow", "wide"),
            P("narrow", "wide"),
            P(("narrow", "wide")),
            P("narrow", "wide"),
            P("narrow", "wide"),
            P(("narrow", "wide")),
            P("narrow", "wide"),
            P("narrow", "wide"),
            P(("narrow", "wide")),
        ),
        out_specs=(
            P("narrow", "wide"),
            P("narrow", "wide"),
            P("narrow", "wide"),
            P(),
            P("narrow", "wide"),
            P("narrow", "wide"),
            P("narrow", "wide"),
            P(),
            P(("narrow", "wide")),
            P(("narrow", "wide")),
            P(("narrow", "wide")),
            P(),
        ),
        check_vma=False,
    )
```

```python
import jax
import jax.numpy as jnp
from jax import lax
from jax.sharding import PartitionSpec as P
from jax.experimental import pallas as pl
from jax.experimental.pallas import tpu as pltpu

BETA_ONE = 0.9
BETA_TWO = 0.999
EPSILON = 1e-06
LEARN_RATE = 0.05
DECAY_RATE = 0.01
CORRECT_FIRST = 1.0 - 0.9**10
CORRECT_SECOND = 1.0 - 0.999**10
LANES = 128


def moments(grad_sum, master, first, second, decay):
    first_new = BETA_ONE * first + (1.0 - BETA_ONE) * grad_sum
    second_new = BETA_TWO * second + (1.0 - BETA_TWO) * grad_sum * grad_sum
    update = (
        first_new / CORRECT_FIRST / (jnp.sqrt(second_new / CORRECT_SECOND) + EPSILON)
        + decay * master
    )
    return (first_new, second_new, update)


def finish(master, update, weight_sq, update_sq):
    trust = jnp.sqrt(weight_sq) / (jnp.sqrt(update_sq) + EPSILON)
    return master - LEARN_RATE * trust * update


def group_sum(x, axis, masks):
    size = lax.axis_size(axis)
    got = [lax.ppermute(x, axis, [(i, i ^ m) for i in range(size)]) for m in masks]
    while len(got) > 1:
        got = [got[i] + got[i + 1] if i + 1 < len(got) else got[i] for i in range(0, len(got), 2)]
    return x + got[0]


def mesh_sum(x):
    x = group_sum(x, "wide", (1,))
    x = group_sum(x, "wide", (2, 4, 6))
    x = group_sum(x, "wide", (8, 16, 24))
    step = 1
    while step < lax.axis_size("narrow"):
        x = group_sum(x, "narrow", (step,))
        step *= 2
    return x


def unpack(whole, up_shape, down_shape):
    n_wide, n_narrow, height, width = whole.shape
    up_rows, up_cols = up_shape
    down_rows, down_cols = down_shape
    per = 2

    def kernel(in_ref, up_ref, down_ref):
        for j in range(per):
            for w in range(n_wide):
                up_ref[up_rows * j : up_rows * (j + 1), up_cols * w : up_cols * (w + 1)] = in_ref[
                    w, j, :up_rows, :up_cols
                ]
                for t in range(3):
                    down_ref[
                        down_rows * j + 16 * t : down_rows * j + 16 * (t + 1),
                        down_cols * w : down_cols * (w + 1),
                    ] = in_ref[w, j, up_rows : up_rows + 16, LANES * t : LANES * (t + 1)]
                for t in range(2):
                    down_ref[
                        down_rows * j + 48 + 8 * t : down_rows * j + 56 + 8 * t,
                        down_cols * w : down_cols * (w + 1),
                    ] = in_ref[w, j, up_rows + 16 : up_rows + 24, LANES * t : LANES * (t + 1)]

    moved = whole.size * 2 + (up_rows * up_cols + down_rows * down_cols) * n_wide * n_narrow * 2
    return pl.pallas_call(
        kernel,
        grid=(n_narrow // per,),
        in_specs=[pl.BlockSpec((n_wide, per, height, width), lambda i: (0, i, 0, 0))],
        out_specs=[
            pl.BlockSpec((per * up_rows, n_wide * up_cols), lambda i: (i, 0)),
            pl.BlockSpec((per * down_rows, n_wide * down_cols), lambda i: (i, 0)),
        ],
        out_shape=[
            jax.ShapeDtypeStruct((n_narrow * up_rows, n_wide * up_cols), jnp.bfloat16),
            jax.ShapeDtypeStruct((n_narrow * down_rows, n_wide * down_cols), jnp.bfloat16),
        ],
        cost_estimate=pl.CostEstimate(flops=0, transcendentals=0, bytes_accessed=moved),
    )(whole)


def body(
    up_grads,
    down_grads,
    gain_grads,
    up_master,
    down_master,
    gain_master,
    up_first,
    down_first,
    gain_first,
    up_second,
    down_second,
    gain_second,
):
    n_wide = lax.axis_size("wide")
    n_narrow = lax.axis_size("narrow")
    up_rows, up_cols = up_master.shape
    down_rows, down_cols = down_master.shape
    gain_cols = gain_master.shape[0]
    up_tiles = -(-up_cols // LANES)
    up_pad = up_tiles * LANES
    up_at = down_rows
    gain_at = up_at + up_rows * up_tiles
    height = -(-(gain_at + 1) // 16) * 16

    down_part = down_grads[0].reshape(down_rows, n_wide, down_cols).transpose(1, 0, 2)
    up_part = up_grads[0].reshape(up_rows, n_wide, up_cols)
    up_part = jnp.pad(up_part, ((0, 0), (0, 0), (0, up_pad - up_cols)))
    up_part = up_part.reshape(up_rows, n_wide, up_tiles, LANES).transpose(1, 0, 2, 3)
    up_part = up_part.reshape(n_wide, up_rows * up_tiles, LANES)
    gain_part = jnp.pad(gain_grads.reshape(n_wide, 1, gain_cols), ((0, 0), (0, 0), (0, LANES - gain_cols)))
    packed = jnp.concatenate(
        [
            down_part,
            up_part,
            gain_part,
            jnp.zeros((n_wide, height - gain_at - 1, LANES), jnp.float32),
        ],
        axis=1,
    )
    received = lax.all_to_all(packed, "wide", 0, 0, tiled=True)
    summed = jnp.sum(received, axis=0)
    down_sum = summed[:down_rows]
    up_sum = summed[up_at:gain_at].reshape(up_rows, up_pad)[:, :up_cols]
    gain_sum = summed[gain_at, :gain_cols]

    up_first_new, up_second_new, up_update = moments(
        up_sum, up_master, up_first, up_second, DECAY_RATE
    )
    down_first_new, down_second_new, down_update = moments(
        down_sum, down_master, down_first, down_second, DECAY_RATE
    )
    gain_first_new, gain_second_new, gain_update = moments(
        gain_sum, gain_master, gain_first, gain_second, 0.0
    )
    partial = jnp.stack(
        [
            jnp.sum(up_master * up_master),
            jnp.sum(down_master * down_master),
            jnp.sum(gain_master * gain_master),
            jnp.sum(up_update * up_update),
            jnp.sum(down_update * down_update),
            jnp.sum(gain_update * gain_update),
            jnp.float32(0.0),
            jnp.float32(0.0),
        ]
    )
    sums = mesh_sum(partial)
    up_master_new = finish(up_master, up_update, sums[0], sums[3])
    down_master_new = finish(down_master, down_update, sums[1], sums[4])
    gain_master_new = finish(gain_master, gain_update, sums[2], sums[5])

    up_low = jnp.pad(up_master_new.astype(jnp.bfloat16), ((0, 0), (0, up_pad - up_cols)))
    down_low = down_master_new.astype(jnp.bfloat16)
    gain_low = jnp.pad(gain_master_new.astype(jnp.bfloat16), (0, LANES - gain_cols))
    gain_low = jnp.pad(gain_low.reshape(1, LANES), ((0, 7), (0, 0)))
    low = jnp.concatenate(
        [
            up_low,
            jnp.concatenate([down_low[0:16], down_low[16:32], down_low[32:48]], axis=1),
            jnp.concatenate([down_low[48:56], down_low[56:64], gain_low], axis=1),
        ]
    )
    rows = lax.all_to_all(
        jnp.broadcast_to(low[None], (n_narrow,) + low.shape), "narrow", 0, 0, tiled=True
    )
    whole = lax.all_gather(rows[None], "wide", axis=0, tiled=True)
    up_weights, down_weights = unpack(whole, up_master.shape, down_master.shape)
    gain_weights = whole[:, :, up_rows + 16, 2 * LANES : 2 * LANES + gain_cols].transpose(1, 0, 2).reshape(-1)
    return (
        up_first_new,
        up_second_new,
        up_master_new,
        up_weights,
        down_first_new,
        down_second_new,
        down_master_new,
        down_weights,
        gain_first_new,
        gain_second_new,
        gain_master_new,
        gain_weights,
    )


def solution(mesh):
    return jax.shard_map(
        body,
        mesh=mesh,
        in_specs=(
            P("wide", "narrow", None),
            P("wide", "narrow", None),
            P("wide", "narrow"),
            P("narrow", "wide"),
            P("narrow", "wide"),
            P(("narrow", "wide")),
            P("narrow", "wide"),
            P("narrow", "wide"),
            P(("narrow", "wide")),
            P("narrow", "wide"),
            P("narrow", "wide"),
            P(("narrow", "wide")),
        ),
        out_specs=(
            P("narrow", "wide"),
            P("narrow", "wide"),
            P("narrow", "wide"),
            P(),
            P("narrow", "wide"),
            P("narrow", "wide"),
            P("narrow", "wide"),
            P(),
            P(("narrow", "wide")),
            P(("narrow", "wide")),
            P(("narrow", "wide")),
            P(),
        ),
        check_vma=False,
    )
```

```python
import jax
import jax.numpy as jnp
from jax import lax
from jax.sharding import PartitionSpec as P
from jax.experimental import pallas as pl
from jax.experimental.pallas import tpu as pltpu

BETA_ONE = 0.9
BETA_TWO = 0.999
EPSILON = 1e-06
LEARN_RATE = 0.05
DECAY_RATE = 0.01
CORRECT_FIRST = 1.0 - 0.9**10
CORRECT_SECOND = 1.0 - 0.999**10
LANES = 128


def moments(grad_sum, master, first, second, decay):
    first_new = BETA_ONE * first + (1.0 - BETA_ONE) * grad_sum
    second_new = BETA_TWO * second + (1.0 - BETA_TWO) * grad_sum * grad_sum
    update = (
        first_new / CORRECT_FIRST / (jnp.sqrt(second_new / CORRECT_SECOND) + EPSILON)
        + decay * master
    )
    return (first_new, second_new, update)


def finish(master, update, weight_sq, update_sq):
    trust = jnp.sqrt(weight_sq) / (jnp.sqrt(update_sq) + EPSILON)
    return master - LEARN_RATE * trust * update


def group_sum(x, axis, masks):
    size = lax.axis_size(axis)
    got = [lax.ppermute(x, axis, [(i, i ^ m) for i in range(size)]) for m in masks]
    while len(got) > 1:
        got = [got[i] + got[i + 1] if i + 1 < len(got) else got[i] for i in range(0, len(got), 2)]
    return x + got[0]


def mesh_sum(x):
    x = group_sum(x, "wide", (1,))
    x = group_sum(x, "wide", (2, 4, 6))
    x = group_sum(x, "wide", (8, 16, 24))
    return x


def unpack(whole, up_shape, down_shape):
    n_wide, n_narrow, height, width = whole.shape
    up_rows, up_cols = up_shape
    down_rows, down_cols = down_shape
    per = 2

    def kernel(in_ref, up_ref, down_ref):
        for j in range(per):
            for w in range(n_wide):
                up_ref[up_rows * j : up_rows * (j + 1), up_cols * w : up_cols * (w + 1)] = in_ref[
                    w, j, :up_rows, :up_cols
                ]
                for t in range(3):
                    down_ref[
                        down_rows * j + 16 * t : down_rows * j + 16 * (t + 1),
                        down_cols * w : down_cols * (w + 1),
                    ] = in_ref[w, j, up_rows : up_rows + 16, LANES * t : LANES * (t + 1)]
                for t in range(2):
                    down_ref[
                        down_rows * j + 48 + 8 * t : down_rows * j + 56 + 8 * t,
                        down_cols * w : down_cols * (w + 1),
                    ] = in_ref[w, j, up_rows + 16 : up_rows + 24, LANES * t : LANES * (t + 1)]

    moved = whole.size * 2 + (up_rows * up_cols + down_rows * down_cols) * n_wide * n_narrow * 2
    return pl.pallas_call(
        kernel,
        grid=(n_narrow // per,),
        in_specs=[pl.BlockSpec((n_wide, per, height, width), lambda i: (0, i, 0, 0))],
        out_specs=[
            pl.BlockSpec((per * up_rows, n_wide * up_cols), lambda i: (i, 0)),
            pl.BlockSpec((per * down_rows, n_wide * down_cols), lambda i: (i, 0)),
        ],
        out_shape=[
            jax.ShapeDtypeStruct((n_narrow * up_rows, n_wide * up_cols), jnp.bfloat16),
            jax.ShapeDtypeStruct((n_narrow * down_rows, n_wide * down_cols), jnp.bfloat16),
        ],
        cost_estimate=pl.CostEstimate(flops=0, transcendentals=0, bytes_accessed=moved),
    )(whole)


def body(
    up_grads,
    down_grads,
    gain_grads,
    up_master,
    down_master,
    gain_master,
    up_first,
    down_first,
    gain_first,
    up_second,
    down_second,
    gain_second,
):
    n_wide = lax.axis_size("wide")
    n_narrow = lax.axis_size("narrow")
    up_rows, up_cols = up_master.shape
    down_rows, down_cols = down_master.shape
    gain_cols = gain_master.shape[0]
    up_tiles = -(-up_cols // LANES)
    up_pad = up_tiles * LANES
    up_at = down_rows
    gain_at = up_at + up_rows * up_tiles
    height = -(-(gain_at + 1) // 16) * 16

    down_part = down_grads[0].reshape(down_rows, n_wide, down_cols).transpose(1, 0, 2)
    up_part = up_grads[0].reshape(up_rows, n_wide, up_cols)
    up_part = jnp.pad(up_part, ((0, 0), (0, 0), (0, up_pad - up_cols)))
    up_part = up_part.reshape(up_rows, n_wide, up_tiles, LANES).transpose(1, 0, 2, 3)
    up_part = up_part.reshape(n_wide, up_rows * up_tiles, LANES)
    gain_part = jnp.pad(gain_grads.reshape(n_wide, 1, gain_cols), ((0, 0), (0, 0), (0, LANES - gain_cols)))
    packed = jnp.concatenate(
        [
            down_part,
            up_part,
            gain_part,
            jnp.zeros((n_wide, height - gain_at - 1, LANES), jnp.float32),
        ],
        axis=1,
    )
    received = lax.all_to_all(packed, "wide", 0, 0, tiled=True)
    summed = jnp.sum(received, axis=0)
    down_sum = summed[:down_rows]
    up_sum = summed[up_at:gain_at].reshape(up_rows, up_pad)[:, :up_cols]
    gain_sum = summed[gain_at, :gain_cols]

    up_first_new, up_second_new, up_update = moments(
        up_sum, up_master, up_first, up_second, DECAY_RATE
    )
    down_first_new, down_second_new, down_update = moments(
        down_sum, down_master, down_first, down_second, DECAY_RATE
    )
    gain_first_new, gain_second_new, gain_update = moments(
        gain_sum, gain_master, gain_first, gain_second, 0.0
    )
    partial = jnp.stack(
        [
            jnp.sum(up_master * up_master),
            jnp.sum(down_master * down_master),
            jnp.sum(gain_master * gain_master),
            jnp.sum(up_update * up_update),
            jnp.sum(down_update * down_update),
            jnp.sum(gain_update * gain_update),
            jnp.float32(0.0),
            jnp.float32(0.0),
        ]
    )

    def as_rows(x):
        return jnp.pad(x, ((0, 0), (0, up_pad - up_cols))).reshape(up_rows * up_tiles, LANES)

    tail = jnp.concatenate(
        [gain_master, gain_update, partial, jnp.zeros((LANES - 2 * gain_cols - 8,), jnp.float32)]
    ).reshape(1, LANES)
    mine = jnp.concatenate(
        [as_rows(up_master), as_rows(up_update), down_master, down_update, tail]
    )
    got = lax.all_to_all(
        jnp.broadcast_to(mine[None], (n_narrow,) + mine.shape), "narrow", 0, 0, tiled=True
    )
    up_span = up_rows * up_tiles
    up_master_all = got[:, :up_span].reshape(n_narrow, up_rows, up_pad)
    up_update_all = got[:, up_span : 2 * up_span].reshape(n_narrow, up_rows, up_pad)
    at = 2 * up_span
    down_master_all = got[:, at : at + down_rows]
    down_update_all = got[:, at + down_rows : at + 2 * down_rows]
    tail_all = got[:, at + 2 * down_rows]
    gain_master_all = tail_all[:, :gain_cols]
    gain_update_all = tail_all[:, gain_cols : 2 * gain_cols]
    narrow_sum = tail_all[0, 2 * gain_cols : 2 * gain_cols + 8]
    for k in range(1, n_narrow):
        narrow_sum = narrow_sum + tail_all[k, 2 * gain_cols : 2 * gain_cols + 8]
    sums = mesh_sum(narrow_sum)
    up_master_new = finish(up_master, up_update, sums[0], sums[3])
    down_master_new = finish(down_master, down_update, sums[1], sums[4])
    gain_master_new = finish(gain_master, gain_update, sums[2], sums[5])

    up_low = finish(up_master_all, up_update_all, sums[0], sums[3]).astype(jnp.bfloat16)
    down_low = finish(down_master_all, down_update_all, sums[1], sums[4]).astype(jnp.bfloat16)
    gain_low = finish(gain_master_all, gain_update_all, sums[2], sums[5]).astype(jnp.bfloat16)
    gain_low = jnp.pad(gain_low, ((0, 0), (0, LANES - gain_cols)))
    gain_low = jnp.pad(gain_low[:, None, :], ((0, 0), (0, 7), (0, 0)))
    rows = jnp.concatenate(
        [
            up_low,
            jnp.concatenate([down_low[:, 0:16], down_low[:, 16:32], down_low[:, 32:48]], axis=2),
            jnp.concatenate([down_low[:, 48:56], down_low[:, 56:64], gain_low], axis=2),
        ],
        axis=1,
    )
    whole = lax.all_gather(rows[None], "wide", axis=0, tiled=True)
    up_weights, down_weights = unpack(whole, up_master.shape, down_master.shape)
    gain_weights = whole[:, :, up_rows + 16, 2 * LANES : 2 * LANES + gain_cols].transpose(1, 0, 2).reshape(-1)
    return (
        up_first_new,
        up_second_new,
        up_master_new,
        up_weights,
        down_first_new,
        down_second_new,
        down_master_new,
        down_weights,
        gain_first_new,
        gain_second_new,
        gain_master_new,
        gain_weights,
    )


def solution(mesh):
    return jax.shard_map(
        body,
        mesh=mesh,
        in_specs=(
            P("wide", "narrow", None),
            P("wide", "narrow", None),
            P("wide", "narrow"),
            P("narrow", "wide"),
            P("narrow", "wide"),
            P(("narrow", "wide")),
            P("narrow", "wide"),
            P("narrow", "wide"),
            P(("narrow", "wide")),
            P("narrow", "wide"),
            P("narrow", "wide"),
            P(("narrow", "wide")),
        ),
        out_specs=(
            P("narrow", "wide"),
            P("narrow", "wide"),
            P("narrow", "wide"),
            P(),
            P("narrow", "wide"),
            P("narrow", "wide"),
            P("narrow", "wide"),
            P(),
            P(("narrow", "wide")),
            P(("narrow", "wide")),
            P(("narrow", "wide")),
            P(),
        ),
        check_vma=False,
    )
```

```python
import jax
import jax.numpy as jnp
from jax import lax
from jax.sharding import PartitionSpec as P
from jax.experimental import pallas as pl
from jax.experimental.pallas import tpu as pltpu

BETA_ONE = 0.9
BETA_TWO = 0.999
EPSILON = 1e-06
LEARN_RATE = 0.05
DECAY_RATE = 0.01
CORRECT_FIRST = 1.0 - 0.9**10
CORRECT_SECOND = 1.0 - 0.999**10
LANES = 128


def moments(grad_sum, master, first, second, decay):
    first_new = BETA_ONE * first + (1.0 - BETA_ONE) * grad_sum
    second_new = BETA_TWO * second + (1.0 - BETA_TWO) * grad_sum * grad_sum
    update = (
        first_new / CORRECT_FIRST / (jnp.sqrt(second_new / CORRECT_SECOND) + EPSILON)
        + decay * master
    )
    return (first_new, second_new, update)


def finish(master, update, weight_sq, update_sq):
    trust = jnp.sqrt(weight_sq) / (jnp.sqrt(update_sq) + EPSILON)
    return master - LEARN_RATE * trust * update


def group_sum(x, axis, masks):
    size = lax.axis_size(axis)
    got = [lax.ppermute(x, axis, [(i, i ^ m) for i in range(size)]) for m in masks]
    while len(got) > 1:
        got = [got[i] + got[i + 1] if i + 1 < len(got) else got[i] for i in range(0, len(got), 2)]
    return x + got[0]


def mesh_sum(x):
    x = group_sum(x, "wide", (1,))
    x = group_sum(x, "wide", (2, 4, 6))
    x = group_sum(x, "wide", (8, 16, 24))
    n_narrow = lax.axis_size("narrow")
    got = lax.all_to_all(jnp.broadcast_to(x[None], (n_narrow,) + x.shape), "narrow", 0, 0, tiled=True)
    total = got[0]
    for k in range(1, n_narrow):
        total = total + got[k]
    return total


def pack(up_g, down_g, gain_g, n_wide, height):
    up_rows, up_cols = up_g.shape[0], up_g.shape[1] // n_wide
    down_rows, down_cols = down_g.shape[0], down_g.shape[1] // n_wide
    gain_cols = gain_g.shape[1] // n_wide
    up_tiles = -(-up_cols // LANES)
    up_at = down_rows
    gain_at = up_at + up_rows * up_tiles
    last = up_at + up_rows * (up_tiles - 1)

    def kernel(up_ref, down_ref, gain_ref, out_ref):
        for w in range(n_wide):
            out_ref[w, last:height, :] = jnp.zeros((height - last, LANES), jnp.float32)
            out_ref[w, :down_rows, :] = down_ref[:, down_cols * w : down_cols * (w + 1)]
            for k in range(up_tiles):
                width = min(LANES, up_cols - LANES * k)
                start = up_cols * w + LANES * k
                out_ref[w, up_at + up_rows * k : up_at + up_rows * (k + 1), :width] = up_ref[
                    :, start : start + width
                ]
            out_ref[w, gain_at : gain_at + 1, :gain_cols] = gain_ref[:, gain_cols * w : gain_cols * (w + 1)]

    moved = (up_g.size + down_g.size + gain_g.size + n_wide * height * LANES) * 4
    return pl.pallas_call(
        kernel,
        in_specs=[pl.BlockSpec(memory_space=pltpu.VMEM)] * 3,
        out_specs=pl.BlockSpec(memory_space=pltpu.VMEM),
        out_shape=jax.ShapeDtypeStruct((n_wide, height, LANES), jnp.float32),
        cost_estimate=pl.CostEstimate(flops=0, transcendentals=0, bytes_accessed=moved),
    )(up_g, down_g, gain_g)


def unpack(whole, up_shape, down_shape):
    n_wide, n_narrow, height, width = whole.shape
    up_rows, up_cols = up_shape
    down_rows, down_cols = down_shape
    per = 2

    def kernel(in_ref, up_ref, down_ref):
        for j in range(per):
            for w in range(n_wide):
                up_ref[up_rows * j : up_rows * (j + 1), up_cols * w : up_cols * (w + 1)] = in_ref[
                    w, j, :up_rows, :up_cols
                ]
                for t in range(3):
                    down_ref[
                        down_rows * j + 16 * t : down_rows * j + 16 * (t + 1),
                        down_cols * w : down_cols * (w + 1),
                    ] = in_ref[w, j, up_rows : up_rows + 16, LANES * t : LANES * (t + 1)]
                for t in range(2):
                    down_ref[
                        down_rows * j + 48 + 8 * t : down_rows * j + 56 + 8 * t,
                        down_cols * w : down_cols * (w + 1),
                    ] = in_ref[w, j, up_rows + 16 : up_rows + 24, LANES * t : LANES * (t + 1)]

    moved = whole.size * 2 + (up_rows * up_cols + down_rows * down_cols) * n_wide * n_narrow * 2
    return pl.pallas_call(
        kernel,
        grid=(n_narrow // per,),
        in_specs=[pl.BlockSpec((n_wide, per, height, width), lambda i: (0, i, 0, 0))],
        out_specs=[
            pl.BlockSpec((per * up_rows, n_wide * up_cols), lambda i: (i, 0)),
            pl.BlockSpec((per * down_rows, n_wide * down_cols), lambda i: (i, 0)),
        ],
        out_shape=[
            jax.ShapeDtypeStruct((n_narrow * up_rows, n_wide * up_cols), jnp.bfloat16),
            jax.ShapeDtypeStruct((n_narrow * down_rows, n_wide * down_cols), jnp.bfloat16),
        ],
        cost_estimate=pl.CostEstimate(flops=0, transcendentals=0, bytes_accessed=moved),
    )(whole)


def body(
    up_grads,
    down_grads,
    gain_grads,
    up_master,
    down_master,
    gain_master,
    up_first,
    down_first,
    gain_first,
    up_second,
    down_second,
    gain_second,
):
    n_wide = lax.axis_size("wide")
    n_narrow = lax.axis_size("narrow")
    up_rows, up_cols = up_master.shape
    down_rows, down_cols = down_master.shape
    gain_cols = gain_master.shape[0]
    up_tiles = -(-up_cols // LANES)
    up_pad = up_tiles * LANES
    up_at = down_rows
    gain_at = up_at + up_rows * up_tiles
    height = -(-(gain_at + 1) // 16) * 16

    packed = pack(up_grads[0], down_grads[0], gain_grads, n_wide, height)
    received = lax.all_to_all(packed, "wide", 0, 0, tiled=True)
    summed = jnp.sum(received, axis=0)
    down_sum = summed[:down_rows]
    up_sum = summed[up_at:gain_at].reshape(up_tiles, up_rows, LANES).transpose(1, 0, 2)
    up_sum = up_sum.reshape(up_rows, up_pad)[:, :up_cols]
    gain_sum = summed[gain_at, :gain_cols]

    up_first_new, up_second_new, up_update = moments(
        up_sum, up_master, up_first, up_second, DECAY_RATE
    )
    down_first_new, down_second_new, down_update = moments(
        down_sum, down_master, down_first, down_second, DECAY_RATE
    )
    gain_first_new, gain_second_new, gain_update = moments(
        gain_sum, gain_master, gain_first, gain_second, 0.0
    )
    partial = jnp.stack(
        [
            jnp.sum(up_master * up_master),
            jnp.sum(down_master * down_master),
            jnp.sum(gain_master * gain_master),
            jnp.sum(up_update * up_update),
            jnp.sum(down_update * down_update),
            jnp.sum(gain_update * gain_update),
            jnp.float32(0.0),
            jnp.float32(0.0),
        ]
    )
    sums = mesh_sum(partial)
    up_master_new = finish(up_master, up_update, sums[0], sums[3])
    down_master_new = finish(down_master, down_update, sums[1], sums[4])
    gain_master_new = finish(gain_master, gain_update, sums[2], sums[5])

    up_low = jnp.pad(up_master_new.astype(jnp.bfloat16), ((0, 0), (0, up_pad - up_cols)))
    down_low = down_master_new.astype(jnp.bfloat16)
    gain_low = jnp.pad(gain_master_new.astype(jnp.bfloat16), (0, LANES - gain_cols))
    gain_low = jnp.pad(gain_low.reshape(1, LANES), ((0, 7), (0, 0)))
    low = jnp.concatenate(
        [
            up_low,
            jnp.concatenate([down_low[0:16], down_low[16:32], down_low[32:48]], axis=1),
            jnp.concatenate([down_low[48:56], down_low[56:64], gain_low], axis=1),
        ]
    )
    rows = lax.all_to_all(
        jnp.broadcast_to(low[None], (n_narrow,) + low.shape), "narrow", 0, 0, tiled=True
    )
    whole = lax.all_gather(rows[None], "wide", axis=0, tiled=True)
    up_weights, down_weights = unpack(whole, up_master.shape, down_master.shape)
    gain_weights = whole[:, :, up_rows + 16, 2 * LANES : 2 * LANES + gain_cols].transpose(1, 0, 2).reshape(-1)
    return (
        up_first_new,
        up_second_new,
        up_master_new,
        up_weights,
        down_first_new,
        down_second_new,
        down_master_new,
        down_weights,
        gain_first_new,
        gain_second_new,
        gain_master_new,
        gain_weights,
    )


def solution(mesh):
    return jax.shard_map(
        body,
        mesh=mesh,
        in_specs=(
            P("wide", "narrow", None),
            P("wide", "narrow", None),
            P("wide", "narrow"),
            P("narrow", "wide"),
            P("narrow", "wide"),
            P(("narrow", "wide")),
            P("narrow", "wide"),
            P("narrow", "wide"),
            P(("narrow", "wide")),
            P("narrow", "wide"),
            P("narrow", "wide"),
            P(("narrow", "wide")),
        ),
        out_specs=(
            P("narrow", "wide"),
            P("narrow", "wide"),
            P("narrow", "wide"),
            P(),
            P("narrow", "wide"),
            P("narrow", "wide"),
            P("narrow", "wide"),
            P(),
            P(("narrow", "wide")),
            P(("narrow", "wide")),
            P(("narrow", "wide")),
            P(),
        ),
        check_vma=False,
    )
```

```python
import jax
import jax.numpy as jnp
from jax import lax
from jax.sharding import PartitionSpec as P
from jax.experimental import pallas as pl
from jax.experimental.pallas import tpu as pltpu

BETA_ONE = 0.9
BETA_TWO = 0.999
EPSILON = 1e-06
LEARN_RATE = 0.05
DECAY_RATE = 0.01
CORRECT_FIRST = 1.0 - 0.9**10
CORRECT_SECOND = 1.0 - 0.999**10
LANES = 128


def moments(grad_sum, master, first, second, decay):
    first_new = BETA_ONE * first + (1.0 - BETA_ONE) * grad_sum
    second_new = BETA_TWO * second + (1.0 - BETA_TWO) * grad_sum * grad_sum
    update = (
        first_new / CORRECT_FIRST / (jnp.sqrt(second_new / CORRECT_SECOND) + EPSILON)
        + decay * master
    )
    return (first_new, second_new, update)


def finish(master, update, weight_sq, update_sq):
    trust = jnp.sqrt(weight_sq) / (jnp.sqrt(update_sq) + EPSILON)
    return master - LEARN_RATE * trust * update


def group_sum(x, axis, masks):
    size = lax.axis_size(axis)
    got = [lax.ppermute(x, axis, [(i, i ^ m) for i in range(size)]) for m in masks]
    while len(got) > 1:
        got = [got[i] + got[i + 1] if i + 1 < len(got) else got[i] for i in range(0, len(got), 2)]
    return x + got[0]


def mesh_sum(x):
    x = group_sum(x, "wide", (1,))
    x = group_sum(x, "wide", (2, 4, 6))
    x = group_sum(x, "wide", (8, 16, 24))
    x = group_sum(x, "narrow", (1,))
    return group_sum(x, "narrow", (2, 4, 6))


def pack(up_g, down_g, gain_g, n_wide, height):
    up_rows, up_cols = up_g.shape[0], up_g.shape[1] // n_wide
    down_rows, down_cols = down_g.shape[0], down_g.shape[1] // n_wide
    gain_cols = gain_g.shape[1] // n_wide
    up_tiles = -(-up_cols // LANES)
    up_at = down_rows
    gain_at = up_at + up_rows * up_tiles
    last = up_at + up_rows * (up_tiles - 1)

    def kernel(up_ref, down_ref, gain_ref, out_ref):
        for w in range(n_wide):
            out_ref[w, last:height, :] = jnp.zeros((height - last, LANES), jnp.float32)
            out_ref[w, :down_rows, :] = down_ref[:, down_cols * w : down_cols * (w + 1)]
            for k in range(up_tiles):
                width = min(LANES, up_cols - LANES * k)
                start = up_cols * w + LANES * k
                out_ref[w, up_at + up_rows * k : up_at + up_rows * (k + 1), :width] = up_ref[
                    :, start : start + width
                ]
            out_ref[w, gain_at : gain_at + 1, :gain_cols] = gain_ref[:, gain_cols * w : gain_cols * (w + 1)]

    moved = (up_g.size + down_g.size + gain_g.size + n_wide * height * LANES) * 4
    return pl.pallas_call(
        kernel,
        in_specs=[pl.BlockSpec(memory_space=pltpu.VMEM)] * 3,
        out_specs=pl.BlockSpec(memory_space=pltpu.VMEM),
        out_shape=jax.ShapeDtypeStruct((n_wide, height, LANES), jnp.float32),
        cost_estimate=pl.CostEstimate(flops=0, transcendentals=0, bytes_accessed=moved),
    )(up_g, down_g, gain_g)


def unpack(whole, up_shape, down_shape):
    n_wide, n_narrow, height, width = whole.shape
    up_rows, up_cols = up_shape
    down_rows, down_cols = down_shape
    per = 2

    def kernel(in_ref, up_ref, down_ref):
        for j in range(per):
            for w in range(n_wide):
                up_ref[up_rows * j : up_rows * (j + 1), up_cols * w : up_cols * (w + 1)] = in_ref[
                    w, j, :up_rows, :up_cols
                ]
                for t in range(3):
                    down_ref[
                        down_rows * j + 16 * t : down_rows * j + 16 * (t + 1),
                        down_cols * w : down_cols * (w + 1),
                    ] = in_ref[w, j, up_rows : up_rows + 16, LANES * t : LANES * (t + 1)]
                for t in range(2):
                    down_ref[
                        down_rows * j + 48 + 8 * t : down_rows * j + 56 + 8 * t,
                        down_cols * w : down_cols * (w + 1),
                    ] = in_ref[w, j, up_rows + 16 : up_rows + 24, LANES * t : LANES * (t + 1)]

    moved = whole.size * 2 + (up_rows * up_cols + down_rows * down_cols) * n_wide * n_narrow * 2
    return pl.pallas_call(
        kernel,
        grid=(n_narrow // per,),
        in_specs=[pl.BlockSpec((n_wide, per, height, width), lambda i: (0, i, 0, 0))],
        out_specs=[
            pl.BlockSpec((per * up_rows, n_wide * up_cols), lambda i: (i, 0)),
            pl.BlockSpec((per * down_rows, n_wide * down_cols), lambda i: (i, 0)),
        ],
        out_shape=[
            jax.ShapeDtypeStruct((n_narrow * up_rows, n_wide * up_cols), jnp.bfloat16),
            jax.ShapeDtypeStruct((n_narrow * down_rows, n_wide * down_cols), jnp.bfloat16),
        ],
        cost_estimate=pl.CostEstimate(flops=0, transcendentals=0, bytes_accessed=moved),
    )(whole)


def body(
    up_grads,
    down_grads,
    gain_grads,
    up_master,
    down_master,
    gain_master,
    up_first,
    down_first,
    gain_first,
    up_second,
    down_second,
    gain_second,
):
    n_wide = lax.axis_size("wide")
    n_narrow = lax.axis_size("narrow")
    up_rows, up_cols = up_master.shape
    down_rows, down_cols = down_master.shape
    gain_cols = gain_master.shape[0]
    up_tiles = -(-up_cols // LANES)
    up_pad = up_tiles * LANES
    up_at = down_rows
    gain_at = up_at + up_rows * up_tiles
    height = -(-(gain_at + 1) // 16) * 16

    packed = pack(up_grads[0], down_grads[0], gain_grads, n_wide, height)
    received = lax.all_to_all(packed, "wide", 0, 0, tiled=True)
    summed = jnp.sum(received, axis=0)
    down_sum = summed[:down_rows]
    up_sum = summed[up_at:gain_at].reshape(up_tiles, up_rows, LANES).transpose(1, 0, 2)
    up_sum = up_sum.reshape(up_rows, up_pad)[:, :up_cols]
    gain_sum = summed[gain_at, :gain_cols]

    up_first_new, up_second_new, up_update = moments(
        up_sum, up_master, up_first, up_second, DECAY_RATE
    )
    down_first_new, down_second_new, down_update = moments(
        down_sum, down_master, down_first, down_second, DECAY_RATE
    )
    gain_first_new, gain_second_new, gain_update = moments(
        gain_sum, gain_master, gain_first, gain_second, 0.0
    )
    def square_sum(x):
        return jnp.sum(x * x, keepdims=True).reshape(1)

    partial = jnp.concatenate(
        [
            square_sum(up_master),
            square_sum(down_master),
            square_sum(gain_master),
            square_sum(up_update),
            square_sum(down_update),
            square_sum(gain_update),
            jnp.zeros((2,), jnp.float32),
        ]
    )
    sums = mesh_sum(partial)
    up_master_new = finish(up_master, up_update, sums[0], sums[3])
    down_master_new = finish(down_master, down_update, sums[1], sums[4])
    gain_master_new = finish(gain_master, gain_update, sums[2], sums[5])

    up_low = jnp.pad(up_master_new.astype(jnp.bfloat16), ((0, 0), (0, up_pad - up_cols)))
    down_low = down_master_new.astype(jnp.bfloat16)
    gain_low = jnp.pad(gain_master_new.astype(jnp.bfloat16), (0, LANES - gain_cols))
    gain_low = jnp.pad(gain_low.reshape(1, LANES), ((0, 7), (0, 0)))
    low = jnp.concatenate(
        [
            up_low,
            jnp.concatenate([down_low[0:16], down_low[16:32], down_low[32:48]], axis=1),
            jnp.concatenate([down_low[48:56], down_low[56:64], gain_low], axis=1),
        ]
    )
    rows = lax.all_to_all(
        jnp.broadcast_to(low[None], (n_narrow,) + low.shape), "narrow", 0, 0, tiled=True
    )
    whole = lax.all_gather(rows[None], "wide", axis=0, tiled=True)
    up_weights, down_weights = unpack(whole, up_master.shape, down_master.shape)
    gain_weights = whole[:, :, up_rows + 16, 2 * LANES : 2 * LANES + gain_cols].transpose(1, 0, 2).reshape(-1)
    return (
        up_first_new,
        up_second_new,
        up_master_new,
        up_weights,
        down_first_new,
        down_second_new,
        down_master_new,
        down_weights,
        gain_first_new,
        gain_second_new,
        gain_master_new,
        gain_weights,
    )


def solution(mesh):
    return jax.shard_map(
        body,
        mesh=mesh,
        in_specs=(
            P("wide", "narrow", None),
            P("wide", "narrow", None),
            P("wide", "narrow"),
            P("narrow", "wide"),
            P("narrow", "wide"),
            P(("narrow", "wide")),
            P("narrow", "wide"),
            P("narrow", "wide"),
            P(("narrow", "wide")),
            P("narrow", "wide"),
            P("narrow", "wide"),
            P(("narrow", "wide")),
        ),
        out_specs=(
            P("narrow", "wide"),
            P("narrow", "wide"),
            P("narrow", "wide"),
            P(),
            P("narrow", "wide"),
            P("narrow", "wide"),
            P("narrow", "wide"),
            P(),
            P(("narrow", "wide")),
            P(("narrow", "wide")),
            P(("narrow", "wide")),
            P(),
        ),
        check_vma=False,
    )
```

```python
import jax
import jax.numpy as jnp
from jax import lax
from jax.sharding import PartitionSpec as P
from jax.experimental import pallas as pl
from jax.experimental.pallas import tpu as pltpu

BETA_ONE = 0.9
BETA_TWO = 0.999
EPSILON = 1e-06
LEARN_RATE = 0.05
DECAY_RATE = 0.01
CORRECT_FIRST = 1.0 - 0.9**10
CORRECT_SECOND = 1.0 - 0.999**10
LANES = 128


def moments(grad_sum, master, first, second, decay):
    first_new = BETA_ONE * first + (1.0 - BETA_ONE) * grad_sum
    second_new = BETA_TWO * second + (1.0 - BETA_TWO) * grad_sum * grad_sum
    update = (
        first_new / CORRECT_FIRST / (jnp.sqrt(second_new / CORRECT_SECOND) + EPSILON)
        + decay * master
    )
    return (first_new, second_new, update)


def finish(master, update, weight_sq, update_sq):
    trust = jnp.sqrt(weight_sq) / (jnp.sqrt(update_sq) + EPSILON)
    return master - LEARN_RATE * trust * update


def group_sum(x, axis, masks):
    size = lax.axis_size(axis)
    got = [lax.ppermute(x, axis, [(i, i ^ m) for i in range(size)]) for m in masks]
    while len(got) > 1:
        got = [got[i] + got[i + 1] if i + 1 < len(got) else got[i] for i in range(0, len(got), 2)]
    return x + got[0]


def mesh_sum(x):
    n = lax.axis_size("wide") * lax.axis_size("narrow")
    got = lax.all_to_all(jnp.broadcast_to(x[None], (n,) + x.shape), ("wide", "narrow"), 0, 0, tiled=True)
    return jnp.sum(got, axis=0)


def pack(up_g, down_g, gain_g, n_wide, height):
    up_rows, up_cols = up_g.shape[0], up_g.shape[1] // n_wide
    down_rows, down_cols = down_g.shape[0], down_g.shape[1] // n_wide
    gain_cols = gain_g.shape[1] // n_wide
    up_tiles = -(-up_cols // LANES)
    up_at = down_rows
    gain_at = up_at + up_rows * up_tiles
    last = up_at + up_rows * (up_tiles - 1)

    def kernel(up_ref, down_ref, gain_ref, out_ref):
        for w in range(n_wide):
            out_ref[w, last:height, :] = jnp.zeros((height - last, LANES), jnp.float32)
            out_ref[w, :down_rows, :] = down_ref[:, down_cols * w : down_cols * (w + 1)]
            for k in range(up_tiles):
                width = min(LANES, up_cols - LANES * k)
                start = up_cols * w + LANES * k
                out_ref[w, up_at + up_rows * k : up_at + up_rows * (k + 1), :width] = up_ref[
                    :, start : start + width
                ]
            out_ref[w, gain_at : gain_at + 1, :gain_cols] = gain_ref[:, gain_cols * w : gain_cols * (w + 1)]

    moved = (up_g.size + down_g.size + gain_g.size + n_wide * height * LANES) * 4
    return pl.pallas_call(
        kernel,
        in_specs=[pl.BlockSpec(memory_space=pltpu.VMEM)] * 3,
        out_specs=pl.BlockSpec(memory_space=pltpu.VMEM),
        out_shape=jax.ShapeDtypeStruct((n_wide, height, LANES), jnp.float32),
        cost_estimate=pl.CostEstimate(flops=0, transcendentals=0, bytes_accessed=moved),
    )(up_g, down_g, gain_g)


def unpack(whole, up_shape, down_shape):
    n_wide, n_narrow, height, width = whole.shape
    up_rows, up_cols = up_shape
    down_rows, down_cols = down_shape
    per = 2

    def kernel(in_ref, up_ref, down_ref):
        for j in range(per):
            for w in range(n_wide):
                up_ref[up_rows * j : up_rows * (j + 1), up_cols * w : up_cols * (w + 1)] = in_ref[
                    w, j, :up_rows, :up_cols
                ]
                for t in range(3):
                    down_ref[
                        down_rows * j + 16 * t : down_rows * j + 16 * (t + 1),
                        down_cols * w : down_cols * (w + 1),
                    ] = in_ref[w, j, up_rows : up_rows + 16, LANES * t : LANES * (t + 1)]
                for t in range(2):
                    down_ref[
                        down_rows * j + 48 + 8 * t : down_rows * j + 56 + 8 * t,
                        down_cols * w : down_cols * (w + 1),
                    ] = in_ref[w, j, up_rows + 16 : up_rows + 24, LANES * t : LANES * (t + 1)]

    moved = whole.size * 2 + (up_rows * up_cols + down_rows * down_cols) * n_wide * n_narrow * 2
    return pl.pallas_call(
        kernel,
        grid=(n_narrow // per,),
        in_specs=[pl.BlockSpec((n_wide, per, height, width), lambda i: (0, i, 0, 0))],
        out_specs=[
            pl.BlockSpec((per * up_rows, n_wide * up_cols), lambda i: (i, 0)),
            pl.BlockSpec((per * down_rows, n_wide * down_cols), lambda i: (i, 0)),
        ],
        out_shape=[
            jax.ShapeDtypeStruct((n_narrow * up_rows, n_wide * up_cols), jnp.bfloat16),
            jax.ShapeDtypeStruct((n_narrow * down_rows, n_wide * down_cols), jnp.bfloat16),
        ],
        cost_estimate=pl.CostEstimate(flops=0, transcendentals=0, bytes_accessed=moved),
    )(whole)


def body(
    up_grads,
    down_grads,
    gain_grads,
    up_master,
    down_master,
    gain_master,
    up_first,
    down_first,
    gain_first,
    up_second,
    down_second,
    gain_second,
):
    n_wide = lax.axis_size("wide")
    n_narrow = lax.axis_size("narrow")
    up_rows, up_cols = up_master.shape
    down_rows, down_cols = down_master.shape
    gain_cols = gain_master.shape[0]
    up_tiles = -(-up_cols // LANES)
    up_pad = up_tiles * LANES
    up_at = down_rows
    gain_at = up_at + up_rows * up_tiles
    height = -(-(gain_at + 1) // 16) * 16

    packed = pack(up_grads[0], down_grads[0], gain_grads, n_wide, height)
    received = lax.all_to_all(packed, "wide", 0, 0, tiled=True)
    summed = jnp.sum(received, axis=0)
    down_sum = summed[:down_rows]
    up_sum = summed[up_at:gain_at].reshape(up_tiles, up_rows, LANES).transpose(1, 0, 2)
    up_sum = up_sum.reshape(up_rows, up_pad)[:, :up_cols]
    gain_sum = summed[gain_at, :gain_cols]

    up_first_new, up_second_new, up_update = moments(
        up_sum, up_master, up_first, up_second, DECAY_RATE
    )
    down_first_new, down_second_new, down_update = moments(
        down_sum, down_master, down_first, down_second, DECAY_RATE
    )
    gain_first_new, gain_second_new, gain_update = moments(
        gain_sum, gain_master, gain_first, gain_second, 0.0
    )
    partial = jnp.stack(
        [
            jnp.sum(up_master * up_master),
            jnp.sum(down_master * down_master),
            jnp.sum(gain_master * gain_master),
            jnp.sum(up_update * up_update),
            jnp.sum(down_update * down_update),
            jnp.sum(gain_update * gain_update),
            jnp.float32(0.0),
            jnp.float32(0.0),
        ]
    )
    sums = mesh_sum(partial)
    up_master_new = finish(up_master, up_update, sums[0], sums[3])
    down_master_new = finish(down_master, down_update, sums[1], sums[4])
    gain_master_new = finish(gain_master, gain_update, sums[2], sums[5])

    up_low = jnp.pad(up_master_new.astype(jnp.bfloat16), ((0, 0), (0, up_pad - up_cols)))
    down_low = down_master_new.astype(jnp.bfloat16)
    gain_low = jnp.pad(gain_master_new.astype(jnp.bfloat16), (0, LANES - gain_cols))
    gain_low = jnp.pad(gain_low.reshape(1, LANES), ((0, 7), (0, 0)))
    low = jnp.concatenate(
        [
            up_low,
            jnp.concatenate([down_low[0:16], down_low[16:32], down_low[32:48]], axis=1),
            jnp.concatenate([down_low[48:56], down_low[56:64], gain_low], axis=1),
        ]
    )
    rows = lax.all_to_all(
        jnp.broadcast_to(low[None], (n_narrow,) + low.shape), "narrow", 0, 0, tiled=True
    )
    whole = lax.all_gather(rows[None], "wide", axis=0, tiled=True)
    up_weights, down_weights = unpack(whole, up_master.shape, down_master.shape)
    gain_weights = whole[:, :, up_rows + 16, 2 * LANES : 2 * LANES + gain_cols].transpose(1, 0, 2).reshape(-1)
    return (
        up_first_new,
        up_second_new,
        up_master_new,
        up_weights,
        down_first_new,
        down_second_new,
        down_master_new,
        down_weights,
        gain_first_new,
        gain_second_new,
        gain_master_new,
        gain_weights,
    )


def solution(mesh):
    return jax.shard_map(
        body,
        mesh=mesh,
        in_specs=(
            P("wide", "narrow", None),
            P("wide", "narrow", None),
            P("wide", "narrow"),
            P("narrow", "wide"),
            P("narrow", "wide"),
            P(("narrow", "wide")),
            P("narrow", "wide"),
            P("narrow", "wide"),
            P(("narrow", "wide")),
            P("narrow", "wide"),
            P("narrow", "wide"),
            P(("narrow", "wide")),
        ),
        out_specs=(
            P("narrow", "wide"),
            P("narrow", "wide"),
            P("narrow", "wide"),
            P(),
            P("narrow", "wide"),
            P("narrow", "wide"),
            P("narrow", "wide"),
            P(),
            P(("narrow", "wide")),
            P(("narrow", "wide")),
            P(("narrow", "wide")),
            P(),
        ),
        check_vma=False,
    )
```

```python
import jax
import jax.numpy as jnp
from jax import lax
from jax.sharding import PartitionSpec as P
from jax.experimental import pallas as pl
from jax.experimental.pallas import tpu as pltpu

BETA_ONE = 0.9
BETA_TWO = 0.999
EPSILON = 1e-06
LEARN_RATE = 0.05
DECAY_RATE = 0.01
CORRECT_FIRST = 1.0 - 0.9**10
CORRECT_SECOND = 1.0 - 0.999**10
LANES = 128


def moments(grad_sum, master, first, second, decay):
    first_new = BETA_ONE * first + (1.0 - BETA_ONE) * grad_sum
    second_new = BETA_TWO * second + (1.0 - BETA_TWO) * grad_sum * grad_sum
    update = (
        first_new / CORRECT_FIRST / (jnp.sqrt(second_new / CORRECT_SECOND) + EPSILON)
        + decay * master
    )
    return (first_new, second_new, update)


def finish(master, update, weight_sq, update_sq):
    trust = jnp.sqrt(weight_sq) / (jnp.sqrt(update_sq) + EPSILON)
    return master - LEARN_RATE * trust * update


def group_sum(x, axis, masks):
    size = lax.axis_size(axis)
    got = [lax.ppermute(x, axis, [(i, i ^ m) for i in range(size)]) for m in masks]
    while len(got) > 1:
        got = [got[i] + got[i + 1] if i + 1 < len(got) else got[i] for i in range(0, len(got), 2)]
    return x + got[0]


def mesh_sum(x):
    n = lax.axis_size("wide") * lax.axis_size("narrow")
    got = lax.all_to_all(jnp.broadcast_to(x[:, None], x.shape + (n,)), ("wide", "narrow"), 1, 1, tiled=True)
    return jnp.sum(got, axis=1)


def pack(up_g, down_g, gain_g, n_wide, height):
    up_rows, up_cols = up_g.shape[0], up_g.shape[1] // n_wide
    down_rows, down_cols = down_g.shape[0], down_g.shape[1] // n_wide
    gain_cols = gain_g.shape[1] // n_wide
    up_tiles = -(-up_cols // LANES)
    up_at = down_rows
    gain_at = up_at + up_rows * up_tiles
    last = up_at + up_rows * (up_tiles - 1)

    def kernel(up_ref, down_ref, gain_ref, out_ref):
        for w in range(n_wide):
            out_ref[w, last:height, :] = jnp.zeros((height - last, LANES), jnp.float32)
            out_ref[w, :down_rows, :] = down_ref[:, down_cols * w : down_cols * (w + 1)]
            for k in range(up_tiles):
                width = min(LANES, up_cols - LANES * k)
                start = up_cols * w + LANES * k
                out_ref[w, up_at + up_rows * k : up_at + up_rows * (k + 1), :width] = up_ref[
                    :, start : start + width
                ]
            out_ref[w, gain_at : gain_at + 1, :gain_cols] = gain_ref[:, gain_cols * w : gain_cols * (w + 1)]

    moved = (up_g.size + down_g.size + gain_g.size + n_wide * height * LANES) * 4
    return pl.pallas_call(
        kernel,
        in_specs=[pl.BlockSpec(memory_space=pltpu.VMEM)] * 3,
        out_specs=pl.BlockSpec(memory_space=pltpu.VMEM),
        out_shape=jax.ShapeDtypeStruct((n_wide, height, LANES), jnp.float32),
        cost_estimate=pl.CostEstimate(flops=0, transcendentals=0, bytes_accessed=moved),
    )(up_g, down_g, gain_g)


def unpack(whole, up_shape, down_shape):
    n_wide, n_narrow, height, width = whole.shape
    up_rows, up_cols = up_shape
    down_rows, down_cols = down_shape
    per = 2

    def kernel(in_ref, up_ref, down_ref):
        for j in range(per):
            for w in range(n_wide):
                up_ref[up_rows * j : up_rows * (j + 1), up_cols * w : up_cols * (w + 1)] = in_ref[
                    w, j, :up_rows, :up_cols
                ]
                for t in range(3):
                    down_ref[
                        down_rows * j + 16 * t : down_rows * j + 16 * (t + 1),
                        down_cols * w : down_cols * (w + 1),
                    ] = in_ref[w, j, up_rows : up_rows + 16, LANES * t : LANES * (t + 1)]
                for t in range(2):
                    down_ref[
                        down_rows * j + 48 + 8 * t : down_rows * j + 56 + 8 * t,
                        down_cols * w : down_cols * (w + 1),
                    ] = in_ref[w, j, up_rows + 16 : up_rows + 24, LANES * t : LANES * (t + 1)]

    moved = whole.size * 2 + (up_rows * up_cols + down_rows * down_cols) * n_wide * n_narrow * 2
    return pl.pallas_call(
        kernel,
        grid=(n_narrow // per,),
        in_specs=[pl.BlockSpec((n_wide, per, height, width), lambda i: (0, i, 0, 0))],
        out_specs=[
            pl.BlockSpec((per * up_rows, n_wide * up_cols), lambda i: (i, 0)),
            pl.BlockSpec((per * down_rows, n_wide * down_cols), lambda i: (i, 0)),
        ],
        out_shape=[
            jax.ShapeDtypeStruct((n_narrow * up_rows, n_wide * up_cols), jnp.bfloat16),
            jax.ShapeDtypeStruct((n_narrow * down_rows, n_wide * down_cols), jnp.bfloat16),
        ],
        cost_estimate=pl.CostEstimate(flops=0, transcendentals=0, bytes_accessed=moved),
    )(whole)


def body(
    up_grads,
    down_grads,
    gain_grads,
    up_master,
    down_master,
    gain_master,
    up_first,
    down_first,
    gain_first,
    up_second,
    down_second,
    gain_second,
):
    n_wide = lax.axis_size("wide")
    n_narrow = lax.axis_size("narrow")
    up_rows, up_cols = up_master.shape
    down_rows, down_cols = down_master.shape
    gain_cols = gain_master.shape[0]
    up_tiles = -(-up_cols // LANES)
    up_pad = up_tiles * LANES
    up_at = down_rows
    gain_at = up_at + up_rows * up_tiles
    height = -(-(gain_at + 1) // 16) * 16

    packed = pack(up_grads[0], down_grads[0], gain_grads, n_wide, height)
    received = lax.all_to_all(packed, "wide", 0, 0, tiled=True)
    summed = jnp.sum(received, axis=0)
    down_sum = summed[:down_rows]
    up_sum = summed[up_at:gain_at].reshape(up_tiles, up_rows, LANES).transpose(1, 0, 2)
    up_sum = up_sum.reshape(up_rows, up_pad)[:, :up_cols]
    gain_sum = summed[gain_at, :gain_cols]

    up_first_new, up_second_new, up_update = moments(
        up_sum, up_master, up_first, up_second, DECAY_RATE
    )
    down_first_new, down_second_new, down_update = moments(
        down_sum, down_master, down_first, down_second, DECAY_RATE
    )
    gain_first_new, gain_second_new, gain_update = moments(
        gain_sum, gain_master, gain_first, gain_second, 0.0
    )
    partial = jnp.stack(
        [
            jnp.sum(up_master * up_master),
            jnp.sum(down_master * down_master),
            jnp.sum(gain_master * gain_master),
            jnp.sum(up_update * up_update),
            jnp.sum(down_update * down_update),
            jnp.sum(gain_update * gain_update),
            jnp.float32(0.0),
            jnp.float32(0.0),
        ]
    )
    sums = mesh_sum(partial)
    up_master_new = finish(up_master, up_update, sums[0], sums[3])
    down_master_new = finish(down_master, down_update, sums[1], sums[4])
    gain_master_new = finish(gain_master, gain_update, sums[2], sums[5])

    up_low = jnp.pad(up_master_new.astype(jnp.bfloat16), ((0, 0), (0, up_pad - up_cols)))
    down_low = down_master_new.astype(jnp.bfloat16)
    gain_low = jnp.pad(gain_master_new.astype(jnp.bfloat16), (0, LANES - gain_cols))
    gain_low = jnp.pad(gain_low.reshape(1, LANES), ((0, 7), (0, 0)))
    low = jnp.concatenate(
        [
            up_low,
            jnp.concatenate([down_low[0:16], down_low[16:32], down_low[32:48]], axis=1),
            jnp.concatenate([down_low[48:56], down_low[56:64], gain_low], axis=1),
        ]
    )
    rows = lax.all_to_all(
        jnp.broadcast_to(low[None], (n_narrow,) + low.shape), "narrow", 0, 0, tiled=True
    )
    whole = lax.all_gather(rows[None], "wide", axis=0, tiled=True)
    up_weights, down_weights = unpack(whole, up_master.shape, down_master.shape)
    gain_weights = whole[:, :, up_rows + 16, 2 * LANES : 2 * LANES + gain_cols].transpose(1, 0, 2).reshape(-1)
    return (
        up_first_new,
        up_second_new,
        up_master_new,
        up_weights,
        down_first_new,
        down_second_new,
        down_master_new,
        down_weights,
        gain_first_new,
        gain_second_new,
        gain_master_new,
        gain_weights,
    )


def solution(mesh):
    return jax.shard_map(
        body,
        mesh=mesh,
        in_specs=(
            P("wide", "narrow", None),
            P("wide", "narrow", None),
            P("wide", "narrow"),
            P("narrow", "wide"),
            P("narrow", "wide"),
            P(("narrow", "wide")),
            P("narrow", "wide"),
            P("narrow", "wide"),
            P(("narrow", "wide")),
            P("narrow", "wide"),
            P("narrow", "wide"),
            P(("narrow", "wide")),
        ),
        out_specs=(
            P("narrow", "wide"),
            P("narrow", "wide"),
            P("narrow", "wide"),
            P(),
            P("narrow", "wide"),
            P("narrow", "wide"),
            P("narrow", "wide"),
            P(),
            P(("narrow", "wide")),
            P(("narrow", "wide")),
            P(("narrow", "wide")),
            P(),
        ),
        check_vma=False,
    )
```
